512 devices in a mesh: sub: 128 (over y, z, core), blk: 4 (over x).
Axes of the slice: x: 4, y: 8, z: 8, core: 2. Of those that a mesh axis runs over, the one named last changes fastest.
Arguments:
- latents: bfloat16 [128, 4, 2, 128], P('sub', 'blk'), may hold values from -6 to 6
- blocks: bfloat16 [128, 4, 2, 6, 128, 128], P('sub', 'blk'), may hold values from -0.21875 to 0.21875
- pattern: int32 [128, 4, 2, 6], P('sub', 'blk'), may hold values from 0 to 5
- linear_term: float32 [128, 4, 2, 128], P('sub', 'blk'), may hold values from -6 to 6
- leaf_front: bfloat16 [128, 4, 512, 512], P('sub', 'blk'), as said below
- live_count: int32 [128, 4], P('sub', 'blk'), may hold values from 1 to 2, as said below
- leaf_map: int32 [128, 4, 2], replicated, may hold values from 0 to 7, all different within a row
- pair_front: bfloat16 [128, 4, 128, 1024], P('sub', 'blk'), as said below
- pair_rhs: float32 [128, 4, 128], P('sub', 'blk'), may hold values from -6 to 6
- pair_map: int32 [64, 4], replicated, may hold values from 0 to 7, all different within a row
- quad_front: bfloat16 [128, 4, 64, 1024], P('sub', 'blk'), as said below
- quad_rhs: float32 [128, 4, 64], P('sub', 'blk'), may hold values from -6 to 6
Outputs:
- gradient: float32 [128, 4, 256], P('sub', 'blk')
- leaf_solve: float32 [128, 4, 256], P('sub', 'blk')
- pair_solve: float32 [128, 4, 64], P('sub', 'blk')
- quad_solve: float32 [128, 4, 32], P('sub', 'blk')
- upper_schur: float32 [128, 4, 32, 512], P('sub', 'blk')
- upper_rhs: float32 [128, 4, 32], P('sub', 'blk')
The draws below stay inside these ranges and needn't reach their ends.
Inputs may be any that keep to these rules, and one draw needn't show every extreme that they name: `leaf_front`: each leaf's matrix is symmetric positive definite. `pair_front`: each pair front, put together from its pieces as the steps say, is symmetric positive definite. `quad_front`: each quad front, put together from its pieces as the steps say, is symmetric positive definite. `live_count`: some leaf has all 2 supernodes live. `leaf_map`: the 2 entries of one leaf differ. `pair_map`: the 4 entries of one pair differ.
All inputs are finite; a program needn't handle non-finite values.
Results may differ from the reference program's by a relative error of at most 0.0003.
Values sent between devices are 32-bit elements; how exact they have to be, the bound alone decides.
No kernel may reach another device: no remote copies, remote signals or barrier semaphores. Data moves between devices by JAX's collectives and lax.ppermute only.
A program may use at most 64 MiB of HBM per device.

```python
import math
import jax
import jax.numpy as jnp
from jax import lax

B = 128
NNZ = 6
IB = 2
UB = 2
K1 = 4
K2 = 4
H1 = 64
H2 = 32
N_SUB = 128
N_BLK = 4


def spd_stack(key, node_count, matrix_size):
    shift = 2.25 + 2.0 / matrix_size ** (2.0 / 3.0)

    def one_matrix(node_key):
        base_key, scale_key = jax.random.split(node_key)
        base = jax.random.normal(base_key, (matrix_size, matrix_size), jnp.float32)
        scales = jnp.exp(jax.random.uniform(scale_key, (matrix_size,), jnp.float32, 0.0, math.log(2.0)))
        symmetric = (base + base.T) * 0.5 ** 0.5 / math.sqrt(matrix_size)
        core = symmetric + shift * jnp.eye(matrix_size, dtype=jnp.float32)
        return (0.5 * scales[:, None] * scales[None, :] * core).astype(jnp.bfloat16)
    return lax.map(one_matrix, jax.random.split(key, node_count))


def draw_leaf_front(key, part):
    matrix_size = (IB + UB) * B
    stacked = spd_stack(jax.random.fold_in(key, 11), N_SUB * N_BLK, matrix_size)
    return stacked.reshape(N_SUB, N_BLK, matrix_size, matrix_size)


def draw_pair_front(key, part):
    matrix_size = 2 * K1 * B
    stacked = spd_stack(jax.random.fold_in(key, 23), N_SUB // 2, matrix_size)
    laid = stacked.reshape(N_SUB // 2, 2, 2, N_BLK, H1, matrix_size).transpose(0, 2, 3, 1, 4, 5)
    return laid.reshape(N_SUB, N_BLK, 2 * H1, matrix_size)


def draw_quad_front(key, part):
    matrix_size = 2 * K2 * B
    stacked = spd_stack(jax.random.fold_in(key, 37), N_SUB // 4, matrix_size)
    laid = stacked.reshape(N_SUB // 4, 2, 4, N_BLK, H2, matrix_size).transpose(0, 2, 3, 1, 4, 5)
    return laid.reshape(N_SUB, N_BLK, 2 * H2, matrix_size)


def draw_live_count(key, part):
    count_key, spot_key = jax.random.split(jax.random.fold_in(key, 5))
    leaves = N_SUB * N_BLK
    counts = jax.random.randint(count_key, (leaves,), 1, IB + 1)
    spot = jax.random.randint(spot_key, (), 0, leaves)
    counts = jnp.where(jnp.arange(leaves) == spot, IB, counts)
    return counts.reshape(N_SUB, N_BLK).astype(jnp.int32)


def touch_ends(values, key, low, top_value):
    dims = values.shape
    place = [jax.random.randint(jax.random.fold_in(key, axis), (), 0, dims[axis]) for axis in range(len(dims))]
    values = values.at[tuple(place)].set(low)
    longest = dims.index(max(dims))
    place[longest] = (place[longest] + 1) % dims[longest]
    return values.at[tuple(place)].set(top_value)


def shard_levels(key, dims, pieces, smallest, top_value):
    level = 1.0
    for axis_at, shards_of in pieces:
        heights = jax.random.uniform(jax.random.fold_in(jax.random.fold_in(key, 6), axis_at), (shards_of,), jnp.float32, smallest / len(pieces), top_value / len(pieces))
        level = level * jnp.repeat(jnp.exp(heights), dims[axis_at] // shards_of).reshape((-1,) + (1,) * (len(dims) - 1 - axis_at))
    return level


def distinct(rng, rows, amount, top, lift):
    order = jax.random.permutation(jax.random.fold_in(rng, 1), amount)
    boost = order
    for power in range(3):
        boost = boost * boost // amount
    boost = boost * lift // amount
    chance = jax.random.randint(jax.random.fold_in(rng, 2), (rows, amount), 0, 4096) + boost
    fixed_rows = jax.random.permutation(jax.random.fold_in(rng, 3), rows)[jnp.arange(amount) % rows]
    chance = jnp.where(jnp.arange(rows)[:, None] == fixed_rows[None, :], 1 << 14, chance)
    merit = chance * amount + jnp.arange(amount)
    return lax.top_k(merit.astype(jnp.int32), top)[1].astype(jnp.int32)


def scatter_about(rng, shape, scale, bound, cuts=(), kind=jnp.bfloat16):
    gain = shard_levels(rng, shape, cuts, -0.22, 0.18) if cuts else 1.0
    entries = jax.random.normal(rng, shape, jnp.float32) * scale * gain
    return jnp.minimum(jnp.maximum(entries, -bound), bound).astype(kind)


def setup_inputs(seed: int = 0) -> dict:
    keys = jax.random.split(jax.random.key(seed), 13)
    return {
        "latents": scatter_about(keys[0], (N_SUB, N_BLK, IB, B), 1.0, 6.0, ((0, 128), (1, 4))),
        "blocks": scatter_about(keys[1], (N_SUB, N_BLK, IB, NNZ, B, B), (NNZ * B) ** -0.5, 0.21875, ((0, 128), (1, 4))),
        "pattern": touch_ends(jax.random.randint(keys[2], (N_SUB, N_BLK, IB, NNZ), 0, 3 * IB), jax.random.fold_in(keys[2], 1), 0, (3 * IB) - 1).astype(jnp.int32),
        "linear_term": scatter_about(keys[3], (N_SUB, N_BLK, IB, B), 1.0, 6.0, ((0, 128), (1, 4)), jnp.float32),
        "leaf_front": draw_leaf_front(jax.random.fold_in(keys[12], 71), 0),
        "live_count": draw_live_count(jax.random.fold_in(keys[12], 71), 0),
        "leaf_map": distinct(keys[6], N_SUB * N_BLK, 2 * K1, UB, 0).reshape((N_SUB, N_BLK, UB)),
        "pair_front": draw_pair_front(jax.random.fold_in(keys[12], 71), 0),
        "pair_rhs": scatter_about(keys[8], (N_SUB, N_BLK, 2 * H1), 1.0, 6.0, ((0, 128), (1, 4)), jnp.float32),
        "pair_map": distinct(keys[9], (N_SUB // 2), 2 * K2, K1, 0),
        "quad_front": draw_quad_front(jax.random.fold_in(keys[12], 71), 0),
        "quad_rhs": scatter_about(keys[11], (N_SUB, N_BLK, 2 * H2), 1.0, 6.0, ((0, 128), (1, 4)), jnp.float32),
    }


exact_setting = lax.Precision.HIGHEST

def lower_triangle_solve(cholesky_factor, right_side):
    return lax.linalg.triangular_solve(cholesky_factor, right_side, left_side=True, lower=True)

def leaf_factor(items):
    front_rows, grad_flat, keep_row = items
    total_size = grad_flat.shape[0]
    whole_front = front_rows.astype(jnp.float32)
    inner_block = whole_front[:total_size, :total_size] * keep_row[:, None] * keep_row[None, :] + jnp.diag(1.0 - keep_row)
    border = whole_front[:total_size, total_size:] * keep_row[:, None]
    corner = whole_front[total_size:, total_size:]
    cholesky_factor = jnp.linalg.cholesky(inner_block)
    solved_rows = lower_triangle_solve(cholesky_factor, grad_flat[:, None])[:, 0]
    panel_row_list = lower_triangle_solve(cholesky_factor, border)
    complement_rows = corner - jnp.dot(panel_row_list.T, panel_row_list, precision=exact_setting)
    carried_right_hand = -jnp.dot(panel_row_list.T, solved_rows, precision=exact_setting)
    return (solved_rows, complement_rows, carried_right_hand)

def assemble(front_rows, load_rows, child_nodes, child_right_hand, child_index_lists):
    child_count = child_nodes.shape[0]
    child_blocks = child_index_lists.shape[1]
    block_width = child_nodes.shape[1] // child_blocks
    total_block_count = front_rows.shape[0] // block_width
    onehot = (child_index_lists[:, :, None] == jnp.arange(total_block_count)[None, None, :]).astype(jnp.float32)
    shaped = child_nodes.reshape(child_count, child_blocks, block_width, child_blocks, block_width)
    rows_done = jnp.einsum('cjk,cjaib->ckaib', onehot, shaped, precision=exact_setting)
    full_add = jnp.einsum('cil,ckaib->kalb', onehot, rows_done, precision=exact_setting)
    whole_front = front_rows + full_add.reshape(front_rows.shape)
    rhs_add = jnp.einsum('cjk,cja->ka', onehot, child_right_hand.reshape(child_count, child_blocks, block_width), precision=exact_setting)
    loaded_rows = load_rows + rhs_add.reshape(-1)
    return (whole_front, loaded_rows)

def eliminate_block(whole_front, loaded_rows, eliminated_width):
    cholesky_factor = jnp.linalg.cholesky(whole_front[:eliminated_width, :eliminated_width])
    solved_rows = lower_triangle_solve(cholesky_factor, loaded_rows[:eliminated_width, None])[:, 0]
    panel_row_list = lower_triangle_solve(cholesky_factor, whole_front[:eliminated_width, eliminated_width:])
    complement_rows = whole_front[eliminated_width:, eliminated_width:] - jnp.dot(panel_row_list.T, panel_row_list, precision=exact_setting)
    carried_right_hand = loaded_rows[eliminated_width:] - jnp.dot(panel_row_list.T, solved_rows, precision=exact_setting)
    return (solved_rows, complement_rows, carried_right_hand)

def tree_node(items):
    front_rows, load_rows, child_nodes, child_right_hand, child_index_lists = items
    whole_front, loaded_rows = assemble(front_rows, load_rows, child_nodes, child_right_hand, child_index_lists)
    return eliminate_block(whole_front, loaded_rows, whole_front.shape[0] // 2)

def reference(latents, blocks, pattern, linear_term, leaf_front, live_count, leaf_map, pair_front, pair_rhs, pair_map, quad_front, quad_rhs):
    interior = IB
    live_mask = (jnp.arange(interior)[None, None, :] < live_count[:, :, None]).astype(jnp.float32)
    masked = latents * live_mask[..., None].astype(jnp.bfloat16)
    block_terms = jnp.einsum('sbjkxy,sbjy->sbjkx', blocks.astype(jnp.float32), masked.astype(jnp.float32), precision=exact_setting)
    onehot = (pattern[..., None] == jnp.arange(3 * interior)[None, None, None, None, :]).astype(jnp.float32)
    spread = jnp.einsum('sbjkd,sbjkx->sbdx', onehot, block_terms, precision=exact_setting)
    own_part = spread[:, :, :interior]
    to_lower = spread[:, :, interior:2 * interior]
    to_upper = spread[:, :, 2 * interior:]
    zero_rows = jnp.zeros_like(own_part[:1])
    from_lower = jnp.concatenate([zero_rows, to_upper[:-1]], 0)
    from_upper = jnp.concatenate([to_lower[1:], zero_rows], 0)
    gradient = (own_part + from_lower + from_upper - linear_term) * live_mask[..., None]
    gradient = gradient.reshape(N_SUB, N_BLK, interior * B)
    keep_rows = jnp.repeat(live_mask, B, axis=2)
    leaves = N_SUB * N_BLK
    leaf_out = lax.map(leaf_factor, (leaf_front.reshape((leaves,) + leaf_front.shape[2:]), gradient.reshape(leaves, -1), keep_rows.reshape(leaves, -1)))
    leaf_solve = leaf_out[0].reshape(N_SUB, N_BLK, interior * B)
    bound_size = UB * B
    pairs = N_SUB // 2
    pair_size = 2 * K1 * B
    pair_rows = pair_front.astype(jnp.float32).reshape(pairs, 2, N_BLK, 2, H1, pair_size).transpose(0, 3, 1, 2, 4, 5).reshape(pairs, pair_size, pair_size)
    pair_loads = pair_rhs.reshape(pairs, 2, N_BLK, 2, H1).transpose(0, 3, 1, 2, 4).reshape(pairs, pair_size)
    pair_children = leaf_out[1].reshape(pairs, 2 * N_BLK, bound_size, bound_size)
    pair_child_rhs = leaf_out[2].reshape(pairs, 2 * N_BLK, bound_size)
    pair_maps = leaf_map.reshape(pairs, 2 * N_BLK, UB)
    pair_out = lax.map(tree_node, (pair_rows, pair_loads, pair_children, pair_child_rhs, pair_maps))
    pair_solve = pair_out[0].reshape(N_SUB, N_BLK, H1)
    quads = N_SUB // 4
    quad_size = 2 * K2 * B
    pass_size = K1 * B
    quad_rows = quad_front.astype(jnp.float32).reshape(quads, 4, N_BLK, 2, H2, quad_size).transpose(0, 3, 1, 2, 4, 5).reshape(quads, quad_size, quad_size)
    quad_loads = quad_rhs.reshape(quads, 4, N_BLK, 2, H2).transpose(0, 3, 1, 2, 4).reshape(quads, quad_size)
    quad_children = pair_out[1].reshape(quads, 2, pass_size, pass_size)
    quad_child_rhs = pair_out[2].reshape(quads, 2, pass_size)
    quad_maps = pair_map.reshape(quads, 2, K1)
    quad_out = lax.map(tree_node, (quad_rows, quad_loads, quad_children, quad_child_rhs, quad_maps))
    quad_solve = quad_out[0].reshape(N_SUB, N_BLK, H2)
    upper_schur = quad_out[1].reshape(N_SUB, N_BLK, H2, K2 * B)
    upper_rhs = quad_out[2].reshape(N_SUB, N_BLK, H2)
    return (gradient, leaf_solve, pair_solve, quad_solve, upper_schur, upper_rhs)
```

```python
import jax
import jax.numpy as jnp
from jax import lax
from jax.sharding import Mesh
from jax.sharding import PartitionSpec as P

exact_setting = lax.Precision.HIGHEST
SUB = ("q", "hi", "lo")
PAIR = ("lo", "blk")
QUAD = ("hi", "lo", "blk")
STEP = 128


def dot(a, b):
    return jnp.dot(a, b, precision=exact_setting)


def halo_exchange(outward, count):
    forward = [(i, i + 1) for i in range(count - 1)]
    backward = [(target, source) for source, target in forward]
    from_lower = lax.ppermute(outward[1], SUB, forward)
    from_upper = lax.ppermute(outward[0], SUB, backward)
    return from_lower, from_upper


def eliminate(rows, width):
    tail = rows.shape[1] - width
    solved = []
    rest = rows
    for start in range(0, width, STEP):
        factor = lax.linalg.cholesky(rest[:STEP, :STEP], symmetrize_input=False)
        upper = lax.linalg.triangular_solve(
            factor, rest[:STEP, STEP:], left_side=True, lower=True
        )
        solved.append(upper[:, upper.shape[1] - tail :])
        remaining = rest.shape[0] - STEP
        if remaining:
            rest = rest[STEP:, STEP:] - dot(upper[:, :remaining].T, upper)
    return jnp.concatenate(solved, 0)


def assemble_add(children, child_rhs, maps, total_blocks):
    count, size = children.shape[0], children.shape[1]
    blocks = maps.shape[1]
    width = size // blocks
    onehot = (maps[:, :, None] == jnp.arange(total_blocks)[None, None, :]).astype(jnp.float32)
    pair_weights = (onehot[:, :, None, :, None] * onehot[:, None, :, None, :]).reshape(
        count * blocks * blocks, total_blocks * total_blocks
    )
    tiles = (
        children.reshape(count, blocks, width, blocks, width)
        .transpose(0, 1, 3, 2, 4)
        .reshape(count * blocks * blocks, width * width)
    )
    placed = dot(pair_weights.T, tiles)
    placed = (
        placed.reshape(total_blocks, total_blocks, width, width)
        .transpose(0, 2, 1, 3)
        .reshape(total_blocks * width, total_blocks * width)
    )
    rhs_add = jnp.einsum(
        "cjm,cja->ma", onehot, child_rhs.reshape(count, blocks, width), precision=exact_setting
    ).reshape(total_blocks * width)
    return placed, rhs_add


def tree_level(front_up, rhs_up, own_front, own_rhs, children, child_rhs, maps, place):
    height = own_front.shape[0] // 2
    size = own_front.shape[1]
    width = size // 2
    total_blocks = size // (children.shape[1] // maps.shape[1])
    placed, rhs_add = assemble_add(children, child_rhs, maps, total_blocks)
    whole_up = front_up + placed[:width]
    load_up = rhs_up + rhs_add[:width]
    low_start = width + place * height
    low_rows = own_front[height:] + lax.dynamic_slice_in_dim(placed, low_start, height, 0)
    low_load = own_rhs[height:] + lax.dynamic_slice_in_dim(rhs_add, low_start, height, 0)
    solved = eliminate(jnp.concatenate([whole_up, load_up[:, None]], 1), width)
    panel = solved[:, :width]
    forward = solved[:, width]
    local_panel = lax.dynamic_slice_in_dim(panel, place * height, height, 1)
    complement = low_rows[:, width:] - dot(local_panel.T, panel)
    carried = low_load - dot(local_panel.T, forward)
    own_solved = lax.dynamic_slice_in_dim(forward, place * height, height, 0)
    return own_solved, complement, carried


def gather_front(front, rhs, axes):
    height = front.shape[0] // 2
    size = front.shape[1]
    piece = jnp.concatenate(
        [front[:height].astype(jnp.float32), jnp.pad(rhs[:height], (0, size - height))[None]], 0
    )
    gathered = lax.all_gather(piece, axes, axis=0, tiled=False)
    front_up = gathered[:, :height, :].reshape(-1, size)
    rhs_up = gathered[:, height, :height].reshape(-1)
    return front_up, rhs_up


def per_device(
    latents,
    blocks,
    pattern,
    linear_term,
    leaf_front,
    live_count,
    leaf_map,
    pair_front,
    pair_rhs,
    pair_map,
    quad_front,
    quad_rhs,
    sub_count,
):
    q_id = lax.axis_index("q")
    hi_id = lax.axis_index("hi")
    lo_id = lax.axis_index("lo")
    blk_id = lax.axis_index("blk")
    blk_count = lax.axis_size("blk")
    sub_id = q_id * 4 + hi_id * 2 + lo_id

    pair_up, pair_up_rhs = gather_front(pair_front[0, 0], pair_rhs[0, 0], PAIR)
    quad_up, quad_up_rhs = gather_front(quad_front[0, 0], quad_rhs[0, 0], QUAD)

    interior = latents.shape[2]
    block_width = latents.shape[3]
    live_mask = (jnp.arange(interior) < live_count[0, 0]).astype(jnp.float32)
    masked = latents[0, 0] * live_mask[:, None].astype(jnp.bfloat16)
    block_terms = jnp.einsum(
        "jkab,jb->jka", blocks[0, 0], masked, preferred_element_type=jnp.float32
    )
    onehot = (pattern[0, 0][:, :, None] == jnp.arange(3 * interior)[None, None, :]).astype(
        jnp.float32
    )
    spread = jnp.einsum("jkd,jka->da", onehot, block_terms, precision=exact_setting)
    outward = jnp.stack([spread[interior : 2 * interior], spread[2 * interior :]])
    from_lower, from_upper = halo_exchange(outward, sub_count)
    gradient = (spread[:interior] + from_lower + from_upper - linear_term[0, 0]) * live_mask[
        :, None
    ]
    total_size = interior * block_width
    grad_flat = gradient.reshape(total_size)

    keep_row = jnp.repeat(live_mask, block_width)
    whole_front = leaf_front[0, 0].astype(jnp.float32)
    inner_block = whole_front[:total_size, :total_size] * keep_row[:, None] * keep_row[
        None, :
    ] + jnp.diag(1.0 - keep_row)
    border = whole_front[:total_size, total_size:] * keep_row[:, None]
    corner = whole_front[total_size:, total_size:]
    solved = eliminate(jnp.concatenate([inner_block, border, grad_flat[:, None]], 1), total_size)
    bound_size = corner.shape[0]
    panel = solved[:, :bound_size]
    leaf_solve = solved[:, bound_size]
    leaf_schur = corner - dot(panel.T, panel)
    leaf_carry = -dot(panel.T, leaf_solve)

    leaf_packed = jnp.concatenate([leaf_schur, leaf_carry[None, :]], 0)
    pair_kids = lax.all_gather(leaf_packed, PAIR, axis=0, tiled=False)
    pair_maps = lax.dynamic_slice_in_dim(leaf_map, sub_id // 2 * 2, 2, 0).reshape(
        -1, leaf_map.shape[2]
    )
    pair_place = blk_count * lo_id + blk_id
    pair_solve, pair_schur, pair_carry = tree_level(
        pair_up,
        pair_up_rhs,
        pair_front[0, 0].astype(jnp.float32),
        pair_rhs[0, 0],
        pair_kids[:, :bound_size, :],
        pair_kids[:, bound_size, :],
        pair_maps,
        pair_place,
    )

    pair_height = pair_schur.shape[0]
    pass_size = pair_schur.shape[1]
    pair_packed = jnp.concatenate(
        [pair_schur, jnp.pad(pair_carry, (0, pass_size - pair_height))[None]], 0
    )
    quad_kids = lax.all_gather(pair_packed, QUAD, axis=0, tiled=False).reshape(
        2, -1, pair_height + 1, pass_size
    )
    quad_children = quad_kids[:, :, :pair_height, :].reshape(2, pass_size, pass_size)
    quad_child_rhs = quad_kids[:, :, pair_height, :pair_height].reshape(2, pass_size)
    quad_maps = lax.dynamic_slice_in_dim(pair_map, sub_id // 4 * 2, 2, 0)
    quad_place = blk_count * (hi_id * 2 + lo_id) + blk_id
    quad_solve, upper_schur, upper_rhs = tree_level(
        quad_up,
        quad_up_rhs,
        quad_front[0, 0].astype(jnp.float32),
        quad_rhs[0, 0],
        quad_children,
        quad_child_rhs,
        quad_maps,
        quad_place,
    )
    return (
        grad_flat[None, None],
        leaf_solve[None, None],
        pair_solve[None, None],
        quad_solve[None, None],
        upper_schur[None, None],
        upper_rhs[None, None],
    )


def solution(mesh):
    sub_count = mesh.shape["sub"]
    blk_count = mesh.shape["blk"]
    grid = mesh.devices.reshape(sub_count // 4, 2, 2, blk_count)
    tree_mesh = Mesh(grid, ("q", "hi", "lo", "blk"))
    placed = (
        P(SUB, "blk", None, None),
        P(SUB, "blk", None, None, None, None),
        P(SUB, "blk", None, None),
        P(SUB, "blk", None, None),
        P(SUB, "blk", None, None),
        P(SUB, "blk"),
        P(),
        P(SUB, "blk", None, None),
        P(SUB, "blk", None),
        P(),
        P(SUB, "blk", None, None),
        P(SUB, "blk", None),
    )

    def body(*args):
        return per_device(*args, sub_count=sub_count)

    return jax.shard_map(
        body,
        mesh=tree_mesh,
        in_specs=placed,
        out_specs=(
            P(SUB, "blk", None),
            P(SUB, "blk", None),
            P(SUB, "blk", None),
            P(SUB, "blk", None),
            P(SUB, "blk", None, None),
            P(SUB, "blk", None),
        ),
        check_vma=False,
    )
```

```python
import jax
import jax.numpy as jnp
from jax import lax
from jax.sharding import Mesh
from jax.sharding import PartitionSpec as P

exact_setting = lax.Precision.HIGHEST
SUB = ("q", "hi", "lo")
PAIR = ("lo", "blk")
QUAD = ("hi", "lo", "blk")
STEP = 128


def dot(a, b):
    return jnp.dot(a, b, precision=exact_setting)


def halo_exchange(outward, count):
    forward = [(i, i + 1) for i in range(count - 1)]
    backward = [(target, source) for source, target in forward]
    from_lower = lax.ppermute(outward[1], SUB, forward)
    from_upper = lax.ppermute(outward[0], SUB, backward)
    return from_lower, from_upper


def eliminate(rows, width):
    tail = rows.shape[1] - width
    solved = []
    rest = rows
    for start in range(0, width, STEP):
        factor = lax.linalg.cholesky(rest[:STEP, :STEP], symmetrize_input=False)
        upper = lax.linalg.triangular_solve(
            factor, rest[:STEP, STEP:], left_side=True, lower=True
        )
        solved.append(upper[:, upper.shape[1] - tail :])
        remaining = rest.shape[0] - STEP
        if remaining:
            rest = rest[STEP:, STEP:] - dot(upper[:, :remaining].T, upper)
    return jnp.concatenate(solved, 0)


def assemble_add(children, child_rhs, maps, total_blocks):
    count, size = children.shape[0], children.shape[1]
    blocks = maps.shape[1]
    width = size // blocks
    onehot = (maps[:, :, None] == jnp.arange(total_blocks)[None, None, :]).astype(jnp.float32)
    pair_weights = (onehot[:, :, None, :, None] * onehot[:, None, :, None, :]).reshape(
        count * blocks * blocks, total_blocks * total_blocks
    )
    tiles = (
        children.reshape(count, blocks, width, blocks, width)
        .transpose(0, 1, 3, 2, 4)
        .reshape(count * blocks * blocks, width * width)
    )
    placed = dot(pair_weights.T, tiles)
    placed = (
        placed.reshape(total_blocks, total_blocks, width, width)
        .transpose(0, 2, 1, 3)
        .reshape(total_blocks * width, total_blocks * width)
    )
    rhs_add = jnp.einsum(
        "cjm,cja->ma", onehot, child_rhs.reshape(count, blocks, width), precision=exact_setting
    ).reshape(total_blocks * width)
    return placed, rhs_add


def tree_level(front_up, rhs_up, own_front, own_rhs, children, child_rhs, maps, place):
    height = own_front.shape[0] // 2
    size = own_front.shape[1]
    width = size // 2
    total_blocks = size // (children.shape[1] // maps.shape[1])
    placed, rhs_add = assemble_add(children, child_rhs, maps, total_blocks)
    whole_up = front_up + placed[:width]
    load_up = rhs_up + rhs_add[:width]
    low_start = width + place * height
    low_rows = own_front[height:] + lax.dynamic_slice_in_dim(placed, low_start, height, 0)
    low_load = own_rhs[height:] + lax.dynamic_slice_in_dim(rhs_add, low_start, height, 0)
    solved = eliminate(jnp.concatenate([whole_up, load_up[:, None]], 1), width)
    panel = solved[:, :width]
    forward = solved[:, width]
    local_panel = lax.dynamic_slice_in_dim(panel, place * height, height, 1)
    complement = low_rows[:, width:] - dot(local_panel.T, panel)
    carried = low_load - dot(local_panel.T, forward)
    own_solved = lax.dynamic_slice_in_dim(forward, place * height, height, 0)
    return own_solved, complement, carried


def gather_front(front, rhs, axes):
    height = front.shape[0] // 2
    size = front.shape[1]
    piece = jnp.concatenate(
        [front[:height].astype(jnp.float32), jnp.pad(rhs[:height], (0, size - height))[None]], 0
    )
    gathered = lax.all_gather(piece, axes, axis=0, tiled=False)
    front_up = gathered[:, :height, :].reshape(-1, size)
    rhs_up = gathered[:, height, :height].reshape(-1)
    return front_up, rhs_up


def per_device(
    latents,
    blocks,
    pattern,
    linear_term,
    leaf_front,
    live_count,
    leaf_map,
    pair_front,
    pair_rhs,
    pair_map,
    quad_front,
    quad_rhs,
    sub_count,
):
    q_id = lax.axis_index("q")
    hi_id = lax.axis_index("hi")
    lo_id = lax.axis_index("lo")
    blk_id = lax.axis_index("blk")
    blk_count = lax.axis_size("blk")
    sub_id = q_id * 4 + hi_id * 2 + lo_id

    pair_up, pair_up_rhs = gather_front(pair_front[0, 0], pair_rhs[0, 0], PAIR)
    quad_up, quad_up_rhs = gather_front(quad_front[0, 0], quad_rhs[0, 0], QUAD)

    interior = latents.shape[2]
    block_width = latents.shape[3]
    live_mask = (jnp.arange(interior) < live_count[0, 0]).astype(jnp.float32)
    masked = latents[0, 0] * live_mask[:, None].astype(jnp.bfloat16)
    block_terms = jnp.einsum(
        "jkab,jb->jka", blocks[0, 0], masked, preferred_element_type=jnp.float32
    )
    onehot = (pattern[0, 0][:, :, None] == jnp.arange(3 * interior)[None, None, :]).astype(
        jnp.float32
    )
    spread = jnp.einsum("jkd,jka->da", onehot, block_terms, precision=exact_setting)
    outward = jnp.stack([spread[interior : 2 * interior], spread[2 * interior :]])
    from_lower, from_upper = halo_exchange(outward, sub_count)
    gradient = (spread[:interior] + from_lower + from_upper - linear_term[0, 0]) * live_mask[
        :, None
    ]
    total_size = interior * block_width
    grad_flat = gradient.reshape(total_size)

    keep_row = jnp.repeat(live_mask, block_width)
    whole_front = leaf_front[0, 0].astype(jnp.float32)
    inner_block = whole_front[:total_size, :total_size] * keep_row[:, None] * keep_row[
        None, :
    ] + jnp.diag(1.0 - keep_row)
    border = whole_front[:total_size, total_size:] * keep_row[:, None]
    corner = whole_front[total_size:, total_size:]
    solved = eliminate(jnp.concatenate([inner_block, border, grad_flat[:, None]], 1), total_size)
    bound_size = corner.shape[0]
    panel = solved[:, :bound_size]
    leaf_solve = solved[:, bound_size]
    leaf_schur = corner - dot(panel.T, panel)
    leaf_carry = -dot(panel.T, leaf_solve)

    leaf_packed = jnp.concatenate([leaf_schur, leaf_carry[None, :]], 0)
    leaf_packed, pair_up, pair_up_rhs, quad_up, quad_up_rhs = lax.optimization_barrier(
        (leaf_packed, pair_up, pair_up_rhs, quad_up, quad_up_rhs)
    )
    pair_kids = lax.all_gather(leaf_packed, PAIR, axis=0, tiled=False)
    pair_maps = lax.dynamic_slice_in_dim(leaf_map, sub_id // 2 * 2, 2, 0).reshape(
        -1, leaf_map.shape[2]
    )
    pair_place = blk_count * lo_id + blk_id
    pair_solve, pair_schur, pair_carry = tree_level(
        pair_up,
        pair_up_rhs,
        pair_front[0, 0].astype(jnp.float32),
        pair_rhs[0, 0],
        pair_kids[:, :bound_size, :],
        pair_kids[:, bound_size, :],
        pair_maps,
        pair_place,
    )

    pair_height = pair_schur.shape[0]
    pass_size = pair_schur.shape[1]
    pair_packed = jnp.concatenate(
        [pair_schur, jnp.pad(pair_carry, (0, pass_size - pair_height))[None]], 0
    )
    quad_kids = lax.all_gather(pair_packed, QUAD, axis=0, tiled=False).reshape(
        2, -1, pair_height + 1, pass_size
    )
    quad_children = quad_kids[:, :, :pair_height, :].reshape(2, pass_size, pass_size)
    quad_child_rhs = quad_kids[:, :, pair_height, :pair_height].reshape(2, pass_size)
    quad_maps = lax.dynamic_slice_in_dim(pair_map, sub_id // 4 * 2, 2, 0)
    quad_place = blk_count * (hi_id * 2 + lo_id) + blk_id
    quad_solve, upper_schur, upper_rhs = tree_level(
        quad_up,
        quad_up_rhs,
        quad_front[0, 0].astype(jnp.float32),
        quad_rhs[0, 0],
        quad_children,
        quad_child_rhs,
        quad_maps,
        quad_place,
    )
    return (
        grad_flat[None, None],
        leaf_solve[None, None],
        pair_solve[None, None],
        quad_solve[None, None],
        upper_schur[None, None],
        upper_rhs[None, None],
    )


def solution(mesh):
    sub_count = mesh.shape["sub"]
    blk_count = mesh.shape["blk"]
    grid = mesh.devices.reshape(sub_count // 4, 2, 2, blk_count)
    tree_mesh = Mesh(grid, ("q", "hi", "lo", "blk"))
    placed = (
        P(SUB, "blk", None, None),
        P(SUB, "blk", None, None, None, None),
        P(SUB, "blk", None, None),
        P(SUB, "blk", None, None),
        P(SUB, "blk", None, None),
        P(SUB, "blk"),
        P(),
        P(SUB, "blk", None, None),
        P(SUB, "blk", None),
        P(),
        P(SUB, "blk", None, None),
        P(SUB, "blk", None),
    )

    def body(*args):
        return per_device(*args, sub_count=sub_count)

    return jax.shard_map(
        body,
        mesh=tree_mesh,
        in_specs=placed,
        out_specs=(
            P(SUB, "blk", None),
            P(SUB, "blk", None),
            P(SUB, "blk", None),
            P(SUB, "blk", None),
            P(SUB, "blk", None, None),
            P(SUB, "blk", None),
        ),
        check_vma=False,
    )
```

```python
import jax
import jax.numpy as jnp
from jax import lax
from jax.sharding import Mesh
from jax.sharding import PartitionSpec as P

exact_setting = lax.Precision.HIGHEST
SUB = ("q", "hi", "lo")
PAIR = ("lo", "blk")
QUAD = ("hi", "lo", "blk")
STEP = 128


def dot(a, b):
    return jnp.dot(a, b, precision=exact_setting)


def halo_exchange(outward, count):
    forward = [(i, i + 1) for i in range(count - 1)]
    backward = [(target, source) for source, target in forward]
    from_lower = lax.ppermute(outward[1], SUB, forward)
    from_upper = lax.ppermute(outward[0], SUB, backward)
    return from_lower, from_upper


def eliminate(rows, width):
    tail = rows.shape[1] - width
    solved = []
    rest = rows
    for start in range(0, width, STEP):
        factor = lax.linalg.cholesky(rest[:STEP, :STEP], symmetrize_input=False)
        upper = lax.linalg.triangular_solve(
            factor, rest[:STEP, STEP:], left_side=True, lower=True
        )
        solved.append(upper[:, upper.shape[1] - tail :])
        remaining = rest.shape[0] - STEP
        if remaining:
            rest = rest[STEP:, STEP:] - dot(upper[:, :remaining].T, upper)
    return jnp.concatenate(solved, 0)


def assemble_add(children, child_rhs, maps, total_blocks):
    count, size = children.shape[0], children.shape[1]
    blocks = maps.shape[1]
    width = size // blocks
    onehot = (maps[:, :, None] == jnp.arange(total_blocks)[None, None, :]).astype(jnp.float32)
    pair_weights = (onehot[:, :, None, :, None] * onehot[:, None, :, None, :]).reshape(
        count * blocks * blocks, total_blocks * total_blocks
    )
    tiles = (
        children.reshape(count, blocks, width, blocks, width)
        .transpose(0, 1, 3, 2, 4)
        .reshape(count * blocks * blocks, width * width)
    )
    placed = dot(pair_weights.T, tiles)
    placed = (
        placed.reshape(total_blocks, total_blocks, width, width)
        .transpose(0, 2, 1, 3)
        .reshape(total_blocks * width, total_blocks * width)
    )
    rhs_add = jnp.einsum(
        "cjm,cja->ma", onehot, child_rhs.reshape(count, blocks, width), precision=exact_setting
    ).reshape(total_blocks * width)
    return placed, rhs_add


def tree_level(front_up, rhs_up, own_front, own_rhs, children, child_rhs, maps, place):
    height = own_front.shape[0] // 2
    size = own_front.shape[1]
    width = size // 2
    total_blocks = size // (children.shape[1] // maps.shape[1])
    placed, rhs_add = assemble_add(children, child_rhs, maps, total_blocks)
    whole_up = front_up + placed[:width]
    load_up = rhs_up + rhs_add[:width]
    low_start = width + place * height
    low_rows = own_front[height:] + lax.dynamic_slice_in_dim(placed, low_start, height, 0)
    low_load = own_rhs[height:] + lax.dynamic_slice_in_dim(rhs_add, low_start, height, 0)
    solved = eliminate(jnp.concatenate([whole_up, load_up[:, None]], 1), width)
    panel = solved[:, :width]
    forward = solved[:, width]
    local_panel = lax.dynamic_slice_in_dim(panel, place * height, height, 1)
    complement = low_rows[:, width:] - dot(local_panel.T, panel)
    carried = low_load - dot(local_panel.T, forward)
    own_solved = lax.dynamic_slice_in_dim(forward, place * height, height, 0)
    return own_solved, complement, carried


def gather_front(front, rhs, axes):
    height = front.shape[0] // 2
    size = front.shape[1]
    piece = jnp.concatenate(
        [front[:height].astype(jnp.float32), jnp.pad(rhs[:height], (0, size - height))[None]], 0
    )
    gathered = lax.all_gather(piece, axes, axis=0, tiled=False)
    front_up = gathered[:, :height, :].reshape(-1, size)
    rhs_up = gathered[:, height, :height].reshape(-1)
    return front_up, rhs_up


def per_device(
    latents,
    blocks,
    pattern,
    linear_term,
    leaf_front,
    live_count,
    leaf_map,
    pair_front,
    pair_rhs,
    pair_map,
    quad_front,
    quad_rhs,
    sub_count,
):
    q_id = lax.axis_index("q")
    hi_id = lax.axis_index("hi")
    lo_id = lax.axis_index("lo")
    blk_id = lax.axis_index("blk")
    blk_count = lax.axis_size("blk")
    sub_id = q_id * 4 + hi_id * 2 + lo_id

    pair_up, pair_up_rhs = gather_front(pair_front[0, 0], pair_rhs[0, 0], PAIR)

    interior = latents.shape[2]
    block_width = latents.shape[3]
    live_mask = (jnp.arange(interior) < live_count[0, 0]).astype(jnp.float32)
    masked = latents[0, 0] * live_mask[:, None].astype(jnp.bfloat16)
    block_terms = jnp.einsum(
        "jkab,jb->jka", blocks[0, 0], masked, preferred_element_type=jnp.float32
    )
    onehot = (pattern[0, 0][:, :, None] == jnp.arange(3 * interior)[None, None, :]).astype(
        jnp.float32
    )
    spread = jnp.einsum("jkd,jka->da", onehot, block_terms, precision=exact_setting)
    outward = jnp.stack([spread[interior : 2 * interior], spread[2 * interior :]])
    from_lower, from_upper = halo_exchange(outward, sub_count)
    gradient = (spread[:interior] + from_lower + from_upper - linear_term[0, 0]) * live_mask[
        :, None
    ]
    total_size = interior * block_width
    grad_flat = gradient.reshape(total_size)

    keep_row = jnp.repeat(live_mask, block_width)
    whole_front = leaf_front[0, 0].astype(jnp.float32)
    inner_block = whole_front[:total_size, :total_size] * keep_row[:, None] * keep_row[
        None, :
    ] + jnp.diag(1.0 - keep_row)
    border = whole_front[:total_size, total_size:] * keep_row[:, None]
    corner = whole_front[total_size:, total_size:]
    solved = eliminate(jnp.concatenate([inner_block, border, grad_flat[:, None]], 1), total_size)
    bound_size = corner.shape[0]
    panel = solved[:, :bound_size]
    leaf_solve = solved[:, bound_size]
    leaf_schur = corner - dot(panel.T, panel)
    leaf_carry = -dot(panel.T, leaf_solve)

    leaf_packed = jnp.concatenate([leaf_schur, leaf_carry[None, :]], 0)
    leaf_packed, pair_up, pair_up_rhs = lax.optimization_barrier(
        (leaf_packed, pair_up, pair_up_rhs)
    )
    pair_kids = lax.all_gather(leaf_packed, PAIR, axis=0, tiled=False)
    quad_own, pair_kids = lax.optimization_barrier((quad_front[0, 0], pair_kids))
    quad_up, quad_up_rhs = gather_front(quad_own, quad_rhs[0, 0], QUAD)
    pair_maps = lax.dynamic_slice_in_dim(leaf_map, sub_id // 2 * 2, 2, 0).reshape(
        -1, leaf_map.shape[2]
    )
    pair_place = blk_count * lo_id + blk_id
    pair_solve, pair_schur, pair_carry = tree_level(
        pair_up,
        pair_up_rhs,
        pair_front[0, 0].astype(jnp.float32),
        pair_rhs[0, 0],
        pair_kids[:, :bound_size, :],
        pair_kids[:, bound_size, :],
        pair_maps,
        pair_place,
    )

    pair_height = pair_schur.shape[0]
    pass_size = pair_schur.shape[1]
    pair_packed = jnp.concatenate(
        [pair_schur, jnp.pad(pair_carry, (0, pass_size - pair_height))[None]], 0
    )
    pair_packed, quad_up, quad_up_rhs = lax.optimization_barrier(
        (pair_packed, quad_up, quad_up_rhs)
    )
    quad_kids = lax.all_gather(pair_packed, QUAD, axis=0, tiled=False).reshape(
        2, -1, pair_height + 1, pass_size
    )
    quad_children = quad_kids[:, :, :pair_height, :].reshape(2, pass_size, pass_size)
    quad_child_rhs = quad_kids[:, :, pair_height, :pair_height].reshape(2, pass_size)
    quad_maps = lax.dynamic_slice_in_dim(pair_map, sub_id // 4 * 2, 2, 0)
    quad_place = blk_count * (hi_id * 2 + lo_id) + blk_id
    quad_solve, upper_schur, upper_rhs = tree_level(
        quad_up,
        quad_up_rhs,
        quad_front[0, 0].astype(jnp.float32),
        quad_rhs[0, 0],
        quad_children,
        quad_child_rhs,
        quad_maps,
        quad_place,
    )
    return (
        grad_flat[None, None],
        leaf_solve[None, None],
        pair_solve[None, None],
        quad_solve[None, None],
        upper_schur[None, None],
        upper_rhs[None, None],
    )


def solution(mesh):
    sub_count = mesh.shape["sub"]
    blk_count = mesh.shape["blk"]
    grid = mesh.devices.reshape(sub_count // 4, 2, 2, blk_count)
    tree_mesh = Mesh(grid, ("q", "hi", "lo", "blk"))
    placed = (
        P(SUB, "blk", None, None),
        P(SUB, "blk", None, None, None, None),
        P(SUB, "blk", None, None),
        P(SUB, "blk", None, None),
        P(SUB, "blk", None, None),
        P(SUB, "blk"),
        P(),
        P(SUB, "blk", None, None),
        P(SUB, "blk", None),
        P(),
        P(SUB, "blk", None, None),
        P(SUB, "blk", None),
    )

    def body(*args):
        return per_device(*args, sub_count=sub_count)

    return jax.shard_map(
        body,
        mesh=tree_mesh,
        in_specs=placed,
        out_specs=(
            P(SUB, "blk", None),
            P(SUB, "blk", None),
            P(SUB, "blk", None),
            P(SUB, "blk", None),
            P(SUB, "blk", None, None),
            P(SUB, "blk", None),
        ),
        check_vma=False,
    )
```

```python
import jax
import jax.numpy as jnp
from jax import lax
from jax.sharding import Mesh
from jax.sharding import PartitionSpec as P

exact_setting = lax.Precision.HIGHEST
SUB = ("q", "hi", "lo")
PAIR = ("lo", "blk")
QUAD = ("hi", "lo", "blk")
STEP = 128


def dot(a, b):
    return jnp.dot(a, b, precision=exact_setting)


def halo_exchange(outward, count):
    forward = [(i, i + 1) for i in range(count - 1)]
    backward = [(target, source) for source, target in forward]
    from_lower = lax.ppermute(outward[1], SUB, forward)
    from_upper = lax.ppermute(outward[0], SUB, backward)
    return from_lower, from_upper


def eliminate(rows, width):
    tail = rows.shape[1] - width
    solved = []
    rest = rows
    for start in range(0, width, STEP):
        factor = lax.linalg.cholesky(rest[:STEP, :STEP], symmetrize_input=False)
        upper = lax.linalg.triangular_solve(
            factor, rest[:STEP, STEP:], left_side=True, lower=True
        )
        solved.append(upper[:, upper.shape[1] - tail :])
        remaining = rest.shape[0] - STEP
        if remaining:
            rest = rest[STEP:, STEP:] - dot(upper[:, :remaining].T, upper)
    return jnp.concatenate(solved, 0)


def assemble_add(children, child_rhs, maps, total_blocks):
    count, size = children.shape[0], children.shape[1]
    blocks = maps.shape[1]
    width = size // blocks
    onehot = (maps[:, :, None] == jnp.arange(total_blocks)[None, None, :]).astype(jnp.float32)
    pair_weights = (onehot[:, :, None, :, None] * onehot[:, None, :, None, :]).reshape(
        count * blocks * blocks, total_blocks * total_blocks
    )
    tiles = (
        children.reshape(count, blocks, width, blocks, width)
        .transpose(0, 1, 3, 2, 4)
        .reshape(count * blocks * blocks, width * width)
    )
    placed = dot(pair_weights.T, tiles)
    placed = (
        placed.reshape(total_blocks, total_blocks, width, width)
        .transpose(0, 2, 1, 3)
        .reshape(total_blocks * width, total_blocks * width)
    )
    rhs_add = jnp.einsum(
        "cjm,cja->ma", onehot, child_rhs.reshape(count, blocks, width), precision=exact_setting
    ).reshape(total_blocks * width)
    return placed, rhs_add


def tree_level(front_up, rhs_up, own_front, own_rhs, children, child_rhs, maps, place):
    height = own_front.shape[0] // 2
    size = own_front.shape[1]
    width = size // 2
    total_blocks = size // (children.shape[1] // maps.shape[1])
    placed, rhs_add = assemble_add(children, child_rhs, maps, total_blocks)
    whole_up = front_up + placed[:width]
    load_up = rhs_up + rhs_add[:width]
    low_start = width + place * height
    low_rows = own_front[height:] + lax.dynamic_slice_in_dim(placed, low_start, height, 0)
    low_load = own_rhs[height:] + lax.dynamic_slice_in_dim(rhs_add, low_start, height, 0)
    solved = eliminate(jnp.concatenate([whole_up, load_up[:, None]], 1), width)
    panel = solved[:, :width]
    forward = solved[:, width]
    local_panel = lax.dynamic_slice_in_dim(panel, place * height, height, 1)
    complement = low_rows[:, width:] - dot(local_panel.T, panel)
    carried = low_load - dot(local_panel.T, forward)
    own_solved = lax.dynamic_slice_in_dim(forward, place * height, height, 0)
    return own_solved, complement, carried


def ring_gather(piece, axis, count):
    own = lax.axis_index(axis)
    received = [piece]
    for shift in range(1, count):
        received.append(
            lax.ppermute(piece, axis, [(i, (i + shift) % count) for i in range(count)])
        )
    flipped = jnp.stack(received[::-1])
    doubled = jnp.concatenate([flipped, flipped], 0)
    return lax.dynamic_slice_in_dim(doubled, (count - 1 - own) % count, count, 0)


def swap_join(stacked, axis):
    partner = lax.ppermute(stacked, axis, [(0, 1), (1, 0)])
    upper = lax.axis_index(axis) == 1
    first = jnp.where(upper, partner, stacked)
    second = jnp.where(upper, stacked, partner)
    return jnp.stack([first, second])


def gather_front(front, rhs, axes):
    height = front.shape[0] // 2
    size = front.shape[1]
    piece = jnp.concatenate(
        [front[:height].astype(jnp.float32), jnp.pad(rhs[:height], (0, size - height))[None]], 0
    )
    gathered = lax.all_gather(piece, axes, axis=0, tiled=False)
    front_up = gathered[:, :height, :].reshape(-1, size)
    rhs_up = gathered[:, height, :height].reshape(-1)
    return front_up, rhs_up


def per_device(
    latents,
    blocks,
    pattern,
    linear_term,
    leaf_front,
    live_count,
    leaf_map,
    pair_front,
    pair_rhs,
    pair_map,
    quad_front,
    quad_rhs,
    sub_count,
):
    q_id = lax.axis_index("q")
    hi_id = lax.axis_index("hi")
    lo_id = lax.axis_index("lo")
    blk_id = lax.axis_index("blk")
    blk_count = lax.axis_size("blk")
    sub_id = q_id * 4 + hi_id * 2 + lo_id

    pair_up, pair_up_rhs = gather_front(pair_front[0, 0], pair_rhs[0, 0], PAIR)

    interior = latents.shape[2]
    block_width = latents.shape[3]
    live_mask = (jnp.arange(interior) < live_count[0, 0]).astype(jnp.float32)
    masked = latents[0, 0] * live_mask[:, None].astype(jnp.bfloat16)
    block_terms = jnp.einsum(
        "jkab,jb->jka", blocks[0, 0], masked, preferred_element_type=jnp.float32
    )
    onehot = (pattern[0, 0][:, :, None] == jnp.arange(3 * interior)[None, None, :]).astype(
        jnp.float32
    )
    spread = jnp.einsum("jkd,jka->da", onehot, block_terms, precision=exact_setting)
    outward = jnp.stack([spread[interior : 2 * interior], spread[2 * interior :]])
    from_lower, from_upper = halo_exchange(outward, sub_count)
    gradient = (spread[:interior] + from_lower + from_upper - linear_term[0, 0]) * live_mask[
        :, None
    ]
    total_size = interior * block_width
    grad_flat = gradient.reshape(total_size)

    keep_row = jnp.repeat(live_mask, block_width)
    whole_front = leaf_front[0, 0].astype(jnp.float32)
    inner_block = whole_front[:total_size, :total_size] * keep_row[:, None] * keep_row[
        None, :
    ] + jnp.diag(1.0 - keep_row)
    border = whole_front[:total_size, total_size:] * keep_row[:, None]
    corner = whole_front[total_size:, total_size:]
    solved = eliminate(jnp.concatenate([inner_block, border, grad_flat[:, None]], 1), total_size)
    bound_size = corner.shape[0]
    panel = solved[:, :bound_size]
    leaf_solve = solved[:, bound_size]
    leaf_schur = corner - dot(panel.T, panel)
    leaf_carry = -dot(panel.T, leaf_solve)

    leaf_packed = jnp.concatenate([leaf_schur, leaf_carry[None, :]], 0)
    leaf_packed, pair_up, pair_up_rhs = lax.optimization_barrier(
        (leaf_packed, pair_up, pair_up_rhs)
    )
    pair_kids = swap_join(ring_gather(leaf_packed, "blk", blk_count), "lo").reshape(
        (-1,) + leaf_packed.shape
    )
    quad_own, pair_kids = lax.optimization_barrier((quad_front[0, 0], pair_kids))
    quad_up, quad_up_rhs = gather_front(quad_own, quad_rhs[0, 0], QUAD)
    pair_maps = lax.dynamic_slice_in_dim(leaf_map, sub_id // 2 * 2, 2, 0).reshape(
        -1, leaf_map.shape[2]
    )
    pair_place = blk_count * lo_id + blk_id
    pair_solve, pair_schur, pair_carry = tree_level(
        pair_up,
        pair_up_rhs,
        pair_front[0, 0].astype(jnp.float32),
        pair_rhs[0, 0],
        pair_kids[:, :bound_size, :],
        pair_kids[:, bound_size, :],
        pair_maps,
        pair_place,
    )

    pair_height = pair_schur.shape[0]
    pass_size = pair_schur.shape[1]
    pair_packed = jnp.concatenate(
        [pair_schur, jnp.pad(pair_carry, (0, pass_size - pair_height))[None]], 0
    )
    pair_packed, quad_up, quad_up_rhs = lax.optimization_barrier(
        (pair_packed, quad_up, quad_up_rhs)
    )
    quad_kids = swap_join(swap_join(ring_gather(pair_packed, "blk", blk_count), "hi"), "lo")
    quad_kids = quad_kids.transpose(1, 0, 2, 3, 4).reshape(2, -1, pair_height + 1, pass_size)
    quad_children = quad_kids[:, :, :pair_height, :].reshape(2, pass_size, pass_size)
    quad_child_rhs = quad_kids[:, :, pair_height, :pair_height].reshape(2, pass_size)
    quad_maps = lax.dynamic_slice_in_dim(pair_map, sub_id // 4 * 2, 2, 0)
    quad_place = blk_count * (hi_id * 2 + lo_id) + blk_id
    quad_solve, upper_schur, upper_rhs = tree_level(
        quad_up,
        quad_up_rhs,
        quad_front[0, 0].astype(jnp.float32),
        quad_rhs[0, 0],
        quad_children,
        quad_child_rhs,
        quad_maps,
        quad_place,
    )
    return (
        grad_flat[None, None],
        leaf_solve[None, None],
        pair_solve[None, None],
        quad_solve[None, None],
        upper_schur[None, None],
        upper_rhs[None, None],
    )


def solution(mesh):
    sub_count = mesh.shape["sub"]
    blk_count = mesh.shape["blk"]
    grid = mesh.devices.reshape(sub_count // 4, 2, 2, blk_count)
    tree_mesh = Mesh(grid, ("q", "hi", "lo", "blk"))
    placed = (
        P(SUB, "blk", None, None),
        P(SUB, "blk", None, None, None, None),
        P(SUB, "blk", None, None),
        P(SUB, "blk", None, None),
        P(SUB, "blk", None, None),
        P(SUB, "blk"),
        P(),
        P(SUB, "blk", None, None),
        P(SUB, "blk", None),
        P(),
        P(SUB, "blk", None, None),
        P(SUB, "blk", None),
    )

    def body(*args):
        return per_device(*args, sub_count=sub_count)

    return jax.shard_map(
        body,
        mesh=tree_mesh,
        in_specs=placed,
        out_specs=(
            P(SUB, "blk", None),
            P(SUB, "blk", None),
            P(SUB, "blk", None),
            P(SUB, "blk", None),
            P(SUB, "blk", None, None),
            P(SUB, "blk", None),
        ),
        check_vma=False,
    )
```

```python
import jax
import jax.numpy as jnp
from jax import lax
from jax.sharding import Mesh
from jax.sharding import PartitionSpec as P

exact_setting = lax.Precision.HIGHEST
SUB = ("q", "hi", "lo")
PAIR = ("lo", "blk")
QUAD = ("hi", "lo", "blk")
STEP = 128


def dot(a, b):
    return jnp.dot(a, b, precision=exact_setting)


def halo_exchange(outward, count):
    forward = [(i, i + 1) for i in range(count - 1)]
    backward = [(target, source) for source, target in forward]
    from_lower = lax.ppermute(outward[1], SUB, forward)
    from_upper = lax.ppermute(outward[0], SUB, backward)
    return from_lower, from_upper


def eliminate(rows, width):
    tail = rows.shape[1] - width
    solved = []
    rest = rows
    for start in range(0, width, STEP):
        factor = lax.linalg.cholesky(rest[:STEP, :STEP], symmetrize_input=False)
        upper = lax.linalg.triangular_solve(
            factor, rest[:STEP, STEP:], left_side=True, lower=True
        )
        solved.append(upper[:, upper.shape[1] - tail :])
        remaining = rest.shape[0] - STEP
        if remaining:
            rest = rest[STEP:, STEP:] - dot(upper[:, :remaining].T, upper)
    return jnp.concatenate(solved, 0)


def assemble_add(children, child_rhs, maps, total_blocks, low_start, height):
    count, size = children.shape[0], children.shape[1]
    blocks = maps.shape[1]
    width = size // blocks
    onehot = (maps[:, :, None] == jnp.arange(total_blocks)[None, None, :]).astype(jnp.float32)
    pair_weights = (onehot[:, :, None, :, None] * onehot[:, None, :, None, :]).reshape(
        count * blocks * blocks, total_blocks * total_blocks
    )
    tiles = (
        children.reshape(count, blocks, width, blocks, width)
        .transpose(0, 1, 3, 2, 4)
        .reshape(count * blocks * blocks, width * width)
    )
    weights = pair_weights.T
    half = total_blocks // 2

    def place_rows(chosen):
        rows = dot(chosen, tiles).reshape(-1, total_blocks, width, width)
        return rows.transpose(0, 2, 1, 3).reshape(-1, total_blocks * width)

    placed_up = place_rows(weights[: half * total_blocks])
    low_block = lax.dynamic_slice_in_dim(
        weights, (low_start // width) * total_blocks, total_blocks, 0
    )
    placed_low = lax.dynamic_slice_in_dim(
        place_rows(low_block), low_start % width, height, 0
    )
    rhs_add = jnp.einsum(
        "cjm,cja->ma", onehot, child_rhs.reshape(count, blocks, width), precision=exact_setting
    ).reshape(total_blocks * width)
    return placed_up, placed_low, rhs_add


def tree_level(front_up, rhs_up, own_front, own_rhs, children, child_rhs, maps, place):
    height = own_front.shape[0] // 2
    size = own_front.shape[1]
    width = size // 2
    total_blocks = size // (children.shape[1] // maps.shape[1])
    low_start = width + place * height
    placed_up, placed_low, rhs_add = assemble_add(
        children, child_rhs, maps, total_blocks, low_start, height
    )
    whole_up = front_up + placed_up
    load_up = rhs_up + rhs_add[:width]
    low_rows = own_front[height:] + placed_low
    low_load = own_rhs[height:] + lax.dynamic_slice_in_dim(rhs_add, low_start, height, 0)
    solved = eliminate(jnp.concatenate([whole_up, load_up[:, None]], 1), width)
    panel = solved[:, :width]
    forward = solved[:, width]
    local_panel = lax.dynamic_slice_in_dim(panel, place * height, height, 1)
    complement = low_rows[:, width:] - dot(local_panel.T, panel)
    carried = low_load - dot(local_panel.T, forward)
    own_solved = lax.dynamic_slice_in_dim(forward, place * height, height, 0)
    return own_solved, complement, carried


def ring_gather(piece, axis, count):
    own = lax.axis_index(axis)
    received = [piece]
    for shift in range(1, count):
        received.append(
            lax.ppermute(piece, axis, [(i, (i + shift) % count) for i in range(count)])
        )
    flipped = jnp.stack(received[::-1])
    doubled = jnp.concatenate([flipped, flipped], 0)
    return lax.dynamic_slice_in_dim(doubled, (count - 1 - own) % count, count, 0)


def swap_join(stacked, axis):
    partner = lax.ppermute(stacked, axis, [(0, 1), (1, 0)])
    upper = lax.axis_index(axis) == 1
    first = jnp.where(upper, partner, stacked)
    second = jnp.where(upper, stacked, partner)
    return jnp.stack([first, second])


def gather_front(front, rhs, axes):
    height = front.shape[0] // 2
    size = front.shape[1]
    piece = jnp.concatenate(
        [front[:height].astype(jnp.float32), jnp.pad(rhs[:height], (0, size - height))[None]], 0
    )
    gathered = lax.all_gather(piece, axes, axis=0, tiled=False)
    front_up = gathered[:, :height, :].reshape(-1, size)
    rhs_up = gathered[:, height, :height].reshape(-1)
    return front_up, rhs_up


def per_device(
    latents,
    blocks,
    pattern,
    linear_term,
    leaf_front,
    live_count,
    leaf_map,
    pair_front,
    pair_rhs,
    pair_map,
    quad_front,
    quad_rhs,
    sub_count,
):
    q_id = lax.axis_index("q")
    hi_id = lax.axis_index("hi")
    lo_id = lax.axis_index("lo")
    blk_id = lax.axis_index("blk")
    blk_count = lax.axis_size("blk")
    sub_id = q_id * 4 + hi_id * 2 + lo_id

    pair_up, pair_up_rhs = gather_front(pair_front[0, 0], pair_rhs[0, 0], PAIR)

    interior = latents.shape[2]
    block_width = latents.shape[3]
    live_mask = (jnp.arange(interior) < live_count[0, 0]).astype(jnp.float32)
    masked = latents[0, 0] * live_mask[:, None].astype(jnp.bfloat16)
    block_terms = jnp.einsum(
        "jkab,jb->jka", blocks[0, 0], masked, preferred_element_type=jnp.float32
    )
    onehot = (pattern[0, 0][:, :, None] == jnp.arange(3 * interior)[None, None, :]).astype(
        jnp.float32
    )
    spread = jnp.einsum("jkd,jka->da", onehot, block_terms, precision=exact_setting)
    outward = jnp.stack([spread[interior : 2 * interior], spread[2 * interior :]])
    from_lower, from_upper = halo_exchange(outward, sub_count)
    gradient = (spread[:interior] + from_lower + from_upper - linear_term[0, 0]) * live_mask[
        :, None
    ]
    total_size = interior * block_width
    grad_flat = gradient.reshape(total_size)

    keep_row = jnp.repeat(live_mask, block_width)
    whole_front = leaf_front[0, 0].astype(jnp.float32)
    inner_block = whole_front[:total_size, :total_size] * keep_row[:, None] * keep_row[
        None, :
    ] + jnp.diag(1.0 - keep_row)
    border = whole_front[:total_size, total_size:] * keep_row[:, None]
    corner = whole_front[total_size:, total_size:]
    solved = eliminate(jnp.concatenate([inner_block, border, grad_flat[:, None]], 1), total_size)
    bound_size = corner.shape[0]
    panel = solved[:, :bound_size]
    leaf_solve = solved[:, bound_size]
    leaf_schur = corner - dot(panel.T, panel)
    leaf_carry = -dot(panel.T, leaf_solve)

    leaf_packed = jnp.concatenate([leaf_schur, leaf_carry[None, :]], 0)
    leaf_packed, pair_up, pair_up_rhs = lax.optimization_barrier(
        (leaf_packed, pair_up, pair_up_rhs)
    )
    pair_kids = swap_join(ring_gather(leaf_packed, "blk", blk_count), "lo").reshape(
        (-1,) + leaf_packed.shape
    )
    quad_own, pair_kids = lax.optimization_barrier((quad_front[0, 0], pair_kids))
    quad_up, quad_up_rhs = gather_front(quad_own, quad_rhs[0, 0], QUAD)
    pair_maps = lax.dynamic_slice_in_dim(leaf_map, sub_id // 2 * 2, 2, 0).reshape(
        -1, leaf_map.shape[2]
    )
    pair_place = blk_count * lo_id + blk_id
    pair_solve, pair_schur, pair_carry = tree_level(
        pair_up,
        pair_up_rhs,
        pair_front[0, 0].astype(jnp.float32),
        pair_rhs[0, 0],
        pair_kids[:, :bound_size, :],
        pair_kids[:, bound_size, :],
        pair_maps,
        pair_place,
    )

    pair_height = pair_schur.shape[0]
    pass_size = pair_schur.shape[1]
    pair_packed = jnp.concatenate(
        [pair_schur, jnp.pad(pair_carry, (0, pass_size - pair_height))[None]], 0
    )
    pair_packed, quad_up, quad_up_rhs = lax.optimization_barrier(
        (pair_packed, quad_up, quad_up_rhs)
    )
    quad_kids = swap_join(ring_gather(swap_join(pair_packed, "hi"), "blk", blk_count), "lo")
    quad_kids = quad_kids.transpose(2, 0, 1, 3, 4).reshape(2, -1, pair_height + 1, pass_size)
    quad_children = quad_kids[:, :, :pair_height, :].reshape(2, pass_size, pass_size)
    quad_child_rhs = quad_kids[:, :, pair_height, :pair_height].reshape(2, pass_size)
    quad_maps = lax.dynamic_slice_in_dim(pair_map, sub_id // 4 * 2, 2, 0)
    quad_place = blk_count * (hi_id * 2 + lo_id) + blk_id
    quad_solve, upper_schur, upper_rhs = tree_level(
        quad_up,
        quad_up_rhs,
        quad_front[0, 0].astype(jnp.float32),
        quad_rhs[0, 0],
        quad_children,
        quad_child_rhs,
        quad_maps,
        quad_place,
    )
    return (
        grad_flat[None, None],
        leaf_solve[None, None],
        pair_solve[None, None],
        quad_solve[None, None],
        upper_schur[None, None],
        upper_rhs[None, None],
    )


def solution(mesh):
    sub_count = mesh.shape["sub"]
    blk_count = mesh.shape["blk"]
    grid = mesh.devices.reshape(sub_count // 4, 2, 2, blk_count)
    tree_mesh = Mesh(grid, ("q", "hi", "lo", "blk"))
    placed = (
        P(SUB, "blk", None, None),
        P(SUB, "blk", None, None, None, None),
        P(SUB, "blk", None, None),
        P(SUB, "blk", None, None),
        P(SUB, "blk", None, None),
        P(SUB, "blk"),
        P(),
        P(SUB, "blk", None, None),
        P(SUB, "blk", None),
        P(),
        P(SUB, "blk", None, None),
        P(SUB, "blk", None),
    )

    def body(*args):
        return per_device(*args, sub_count=sub_count)

    return jax.shard_map(
        body,
        mesh=tree_mesh,
        in_specs=placed,
        out_specs=(
            P(SUB, "blk", None),
            P(SUB, "blk", None),
            P(SUB, "blk", None),
            P(SUB, "blk", None),
            P(SUB, "blk", None, None),
            P(SUB, "blk", None),
        ),
        check_vma=False,
    )
```

```python
import jax
import jax.numpy as jnp
from jax import lax
from jax.sharding import Mesh
from jax.sharding import PartitionSpec as P

exact_setting = lax.Precision.HIGHEST
SUB = ("q", "hi", "lo")
PAIR = ("lo", "blk")
QUAD = ("hi", "lo", "blk")
STEP = 128


def dot(a, b):
    return jnp.dot(a, b, precision=exact_setting)


def halo_exchange(outward, count):
    forward = [(i, i + 1) for i in range(count - 1)]
    backward = [(target, source) for source, target in forward]
    from_lower = lax.ppermute(outward[1], SUB, forward)
    from_upper = lax.ppermute(outward[0], SUB, backward)
    return from_lower, from_upper


def eliminate(rows, width):
    tail = rows.shape[1] - width
    solved = []
    rest = rows
    for start in range(0, width, STEP):
        factor = lax.linalg.cholesky(rest[:STEP, :STEP], symmetrize_input=False)
        upper = lax.linalg.triangular_solve(
            factor, rest[:STEP, STEP:], left_side=True, lower=True
        )
        solved.append(upper[:, upper.shape[1] - tail :])
        remaining = rest.shape[0] - STEP
        if remaining:
            rest = rest[STEP:, STEP:] - dot(upper[:, :remaining].T, upper)
    return jnp.concatenate(solved, 0)


def eliminate_loop(rows, width):
    row_count, col_count = rows.shape
    tail = col_count - width
    columns = jnp.arange(col_count)

    def step(index, carry):
        rest, solved = carry
        start = index * STEP
        panel_rows = lax.dynamic_slice_in_dim(rest, start, STEP, 0)
        diagonal = lax.dynamic_slice_in_dim(panel_rows, start, STEP, 1)
        factor = lax.linalg.cholesky(diagonal, symmetrize_input=False)
        upper = lax.linalg.triangular_solve(factor, panel_rows, left_side=True, lower=True)
        upper = jnp.where((columns >= start + STEP)[None, :], upper, 0.0)
        solved = lax.dynamic_update_slice_in_dim(solved, upper[:, width:], start, 0)
        rest = rest - dot(upper[:, :row_count].T, upper)
        return rest, solved

    start_solved = jnp.zeros((width, tail), rows.dtype)
    _, solved = lax.fori_loop(0, width // STEP, step, (rows, start_solved))
    return solved


def assemble_add(children, child_rhs, maps, total_blocks, low_start, height):
    count, size = children.shape[0], children.shape[1]
    blocks = maps.shape[1]
    width = size // blocks
    onehot = (maps[:, :, None] == jnp.arange(total_blocks)[None, None, :]).astype(jnp.float32)
    pair_weights = (onehot[:, :, None, :, None] * onehot[:, None, :, None, :]).reshape(
        count * blocks * blocks, total_blocks * total_blocks
    )
    tiles = (
        children.reshape(count, blocks, width, blocks, width)
        .transpose(0, 1, 3, 2, 4)
        .reshape(count * blocks * blocks, width * width)
    )
    weights = pair_weights.T
    half = total_blocks // 2

    def place_rows(chosen):
        rows = dot(chosen, tiles).reshape(-1, total_blocks, width, width)
        return rows.transpose(0, 2, 1, 3).reshape(-1, total_blocks * width)

    placed_up = place_rows(weights[: half * total_blocks])
    low_block = lax.dynamic_slice_in_dim(
        weights, (low_start // width) * total_blocks, total_blocks, 0
    )
    placed_low = lax.dynamic_slice_in_dim(
        place_rows(low_block), low_start % width, height, 0
    )
    rhs_add = jnp.einsum(
        "cjm,cja->ma", onehot, child_rhs.reshape(count, blocks, width), precision=exact_setting
    ).reshape(total_blocks * width)
    return placed_up, placed_low, rhs_add


def tree_level(front_up, rhs_up, own_front, own_rhs, children, child_rhs, maps, place):
    height = own_front.shape[0] // 2
    size = own_front.shape[1]
    width = size // 2
    total_blocks = size // (children.shape[1] // maps.shape[1])
    low_start = width + place * height
    placed_up, placed_low, rhs_add = assemble_add(
        children, child_rhs, maps, total_blocks, low_start, height
    )
    whole_up = front_up + placed_up
    load_up = rhs_up + rhs_add[:width]
    low_rows = own_front[height:] + placed_low
    low_load = own_rhs[height:] + lax.dynamic_slice_in_dim(rhs_add, low_start, height, 0)
    solved = eliminate_loop(jnp.concatenate([whole_up, load_up[:, None]], 1), width)
    panel = solved[:, :width]
    forward = solved[:, width]
    local_panel = lax.dynamic_slice_in_dim(panel, place * height, height, 1)
    complement = low_rows[:, width:] - dot(local_panel.T, panel)
    carried = low_load - dot(local_panel.T, forward)
    own_solved = lax.dynamic_slice_in_dim(forward, place * height, height, 0)
    return own_solved, complement, carried


def ring_gather(piece, axis, count):
    own = lax.axis_index(axis)
    received = [piece]
    for shift in range(1, count):
        received.append(
            lax.ppermute(piece, axis, [(i, (i + shift) % count) for i in range(count)])
        )
    flipped = jnp.stack(received[::-1])
    doubled = jnp.concatenate([flipped, flipped], 0)
    return lax.dynamic_slice_in_dim(doubled, (count - 1 - own) % count, count, 0)


def swap_join(stacked, axis):
    partner = lax.ppermute(stacked, axis, [(0, 1), (1, 0)])
    upper = lax.axis_index(axis) == 1
    first = jnp.where(upper, partner, stacked)
    second = jnp.where(upper, stacked, partner)
    return jnp.stack([first, second])


def gather_front(front, rhs, axes):
    height = front.shape[0] // 2
    size = front.shape[1]
    piece = jnp.concatenate(
        [front[:height].astype(jnp.float32), jnp.pad(rhs[:height], (0, size - height))[None]], 0
    )
    gathered = lax.all_gather(piece, axes, axis=0, tiled=False)
    front_up = gathered[:, :height, :].reshape(-1, size)
    rhs_up = gathered[:, height, :height].reshape(-1)
    return front_up, rhs_up


def per_device(
    latents,
    blocks,
    pattern,
    linear_term,
    leaf_front,
    live_count,
    leaf_map,
    pair_front,
    pair_rhs,
    pair_map,
    quad_front,
    quad_rhs,
    sub_count,
):
    q_id = lax.axis_index("q")
    hi_id = lax.axis_index("hi")
    lo_id = lax.axis_index("lo")
    blk_id = lax.axis_index("blk")
    blk_count = lax.axis_size("blk")
    sub_id = q_id * 4 + hi_id * 2 + lo_id

    pair_up, pair_up_rhs = gather_front(pair_front[0, 0], pair_rhs[0, 0], PAIR)

    interior = latents.shape[2]
    block_width = latents.shape[3]
    live_mask = (jnp.arange(interior) < live_count[0, 0]).astype(jnp.float32)
    masked = latents[0, 0] * live_mask[:, None].astype(jnp.bfloat16)
    block_terms = jnp.einsum(
        "jkab,jb->jka", blocks[0, 0], masked, preferred_element_type=jnp.float32
    )
    onehot = (pattern[0, 0][:, :, None] == jnp.arange(3 * interior)[None, None, :]).astype(
        jnp.float32
    )
    spread = jnp.einsum("jkd,jka->da", onehot, block_terms, precision=exact_setting)
    outward = jnp.stack([spread[interior : 2 * interior], spread[2 * interior :]])
    from_lower, from_upper = halo_exchange(outward, sub_count)
    gradient = (spread[:interior] + from_lower + from_upper - linear_term[0, 0]) * live_mask[
        :, None
    ]
    total_size = interior * block_width
    grad_flat = gradient.reshape(total_size)

    keep_row = jnp.repeat(live_mask, block_width)
    whole_front = leaf_front[0, 0].astype(jnp.float32)
    inner_block = whole_front[:total_size, :total_size] * keep_row[:, None] * keep_row[
        None, :
    ] + jnp.diag(1.0 - keep_row)
    border = whole_front[:total_size, total_size:] * keep_row[:, None]
    corner = whole_front[total_size:, total_size:]
    solved = eliminate(jnp.concatenate([inner_block, border, grad_flat[:, None]], 1), total_size)
    bound_size = corner.shape[0]
    panel = solved[:, :bound_size]
    leaf_solve = solved[:, bound_size]
    leaf_schur = corner - dot(panel.T, panel)
    leaf_carry = -dot(panel.T, leaf_solve)

    leaf_packed = jnp.concatenate([leaf_schur, leaf_carry[None, :]], 0)
    leaf_packed, pair_up, pair_up_rhs = lax.optimization_barrier(
        (leaf_packed, pair_up, pair_up_rhs)
    )
    pair_kids = swap_join(ring_gather(leaf_packed, "blk", blk_count), "lo").reshape(
        (-1,) + leaf_packed.shape
    )
    quad_own, pair_kids = lax.optimization_barrier((quad_front[0, 0], pair_kids))
    quad_up, quad_up_rhs = gather_front(quad_own, quad_rhs[0, 0], QUAD)
    pair_maps = lax.dynamic_slice_in_dim(leaf_map, sub_id // 2 * 2, 2, 0).reshape(
        -1, leaf_map.shape[2]
    )
    pair_place = blk_count * lo_id + blk_id
    pair_solve, pair_schur, pair_carry = tree_level(
        pair_up,
        pair_up_rhs,
        pair_front[0, 0].astype(jnp.float32),
        pair_rhs[0, 0],
        pair_kids[:, :bound_size, :],
        pair_kids[:, bound_size, :],
        pair_maps,
        pair_place,
    )

    pair_height = pair_schur.shape[0]
    pass_size = pair_schur.shape[1]
    pair_packed = jnp.concatenate(
        [pair_schur, jnp.pad(pair_carry, (0, pass_size - pair_height))[None]], 0
    )
    pair_packed, quad_up, quad_up_rhs = lax.optimization_barrier(
        (pair_packed, quad_up, quad_up_rhs)
    )
    quad_kids = swap_join(ring_gather(swap_join(pair_packed, "hi"), "blk", blk_count), "lo")
    quad_kids = quad_kids.transpose(2, 0, 1, 3, 4).reshape(2, -1, pair_height + 1, pass_size)
    quad_children = quad_kids[:, :, :pair_height, :].reshape(2, pass_size, pass_size)
    quad_child_rhs = quad_kids[:, :, pair_height, :pair_height].reshape(2, pass_size)
    quad_maps = lax.dynamic_slice_in_dim(pair_map, sub_id // 4 * 2, 2, 0)
    quad_place = blk_count * (hi_id * 2 + lo_id) + blk_id
    quad_solve, upper_schur, upper_rhs = tree_level(
        quad_up,
        quad_up_rhs,
        quad_front[0, 0].astype(jnp.float32),
        quad_rhs[0, 0],
        quad_children,
        quad_child_rhs,
        quad_maps,
        quad_place,
    )
    return (
        grad_flat[None, None],
        leaf_solve[None, None],
        pair_solve[None, None],
        quad_solve[None, None],
        upper_schur[None, None],
        upper_rhs[None, None],
    )


def solution(mesh):
    sub_count = mesh.shape["sub"]
    blk_count = mesh.shape["blk"]
    grid = mesh.devices.reshape(sub_count // 4, 2, 2, blk_count)
    tree_mesh = Mesh(grid, ("q", "hi", "lo", "blk"))
    placed = (
        P(SUB, "blk", None, None),
        P(SUB, "blk", None, None, None, None),
        P(SUB, "blk", None, None),
        P(SUB, "blk", None, None),
        P(SUB, "blk", None, None),
        P(SUB, "blk"),
        P(),
        P(SUB, "blk", None, None),
        P(SUB, "blk", None),
        P(),
        P(SUB, "blk", None, None),
        P(SUB, "blk", None),
    )

    def body(*args):
        return per_device(*args, sub_count=sub_count)

    return jax.shard_map(
        body,
        mesh=tree_mesh,
        in_specs=placed,
        out_specs=(
            P(SUB, "blk", None),
            P(SUB, "blk", None),
            P(SUB, "blk", None),
            P(SUB, "blk", None),
            P(SUB, "blk", None, None),
            P(SUB, "blk", None),
        ),
        check_vma=False,
    )
```

```python
import jax
import jax.numpy as jnp
from jax import lax
from jax.sharding import Mesh
from jax.sharding import PartitionSpec as P

exact_setting = lax.Precision.HIGHEST
SUB = ("q", "hi", "lo")
PAIR = ("lo", "blk")
QUAD = ("hi", "lo", "blk")
STEP = 128


def dot(a, b):
    return jnp.dot(a, b, precision=exact_setting)


def update_dot(a, b):
    return jnp.dot(a, b, precision=lax.Precision.HIGH, preferred_element_type=jnp.float32)


def halo_exchange(outward, count):
    forward = [(i, i + 1) for i in range(count - 1)]
    backward = [(target, source) for source, target in forward]
    from_lower = lax.ppermute(outward[1], SUB, forward)
    from_upper = lax.ppermute(outward[0], SUB, backward)
    return from_lower, from_upper


def eliminate(rows, width):
    tail = rows.shape[1] - width
    solved = []
    rest = rows
    for start in range(0, width, STEP):
        factor = lax.linalg.cholesky(rest[:STEP, :STEP], symmetrize_input=False)
        upper = lax.linalg.triangular_solve(
            factor, rest[:STEP, STEP:], left_side=True, lower=True
        )
        solved.append(upper[:, upper.shape[1] - tail :])
        remaining = rest.shape[0] - STEP
        if remaining:
            rest = rest[STEP:, STEP:] - update_dot(upper[:, :remaining].T, upper)
    return jnp.concatenate(solved, 0)


def assemble_add(children, child_rhs, maps, total_blocks, low_start, height):
    count, size = children.shape[0], children.shape[1]
    blocks = maps.shape[1]
    width = size // blocks
    onehot = (maps[:, :, None] == jnp.arange(total_blocks)[None, None, :]).astype(jnp.float32)
    pair_weights = (onehot[:, :, None, :, None] * onehot[:, None, :, None, :]).reshape(
        count * blocks * blocks, total_blocks * total_blocks
    )
    tiles = (
        children.reshape(count, blocks, width, blocks, width)
        .transpose(0, 1, 3, 2, 4)
        .reshape(count * blocks * blocks, width * width)
    )
    weights = pair_weights.T
    half = total_blocks // 2

    def place_rows(chosen):
        rows = dot(chosen, tiles).reshape(-1, total_blocks, width, width)
        return rows.transpose(0, 2, 1, 3).reshape(-1, total_blocks * width)

    placed_up = place_rows(weights[: half * total_blocks])
    low_block = lax.dynamic_slice_in_dim(
        weights, (low_start // width) * total_blocks, total_blocks, 0
    )
    placed_low = lax.dynamic_slice_in_dim(
        place_rows(low_block), low_start % width, height, 0
    )
    rhs_add = jnp.einsum(
        "cjm,cja->ma", onehot, child_rhs.reshape(count, blocks, width), precision=exact_setting
    ).reshape(total_blocks * width)
    return placed_up, placed_low, rhs_add


def tree_level(front_up, rhs_up, own_front, own_rhs, children, child_rhs, maps, place):
    height = own_front.shape[0] // 2
    size = own_front.shape[1]
    width = size // 2
    total_blocks = size // (children.shape[1] // maps.shape[1])
    low_start = width + place * height
    placed_up, placed_low, rhs_add = assemble_add(
        children, child_rhs, maps, total_blocks, low_start, height
    )
    whole_up = front_up + placed_up
    load_up = rhs_up + rhs_add[:width]
    low_rows = own_front[height:] + placed_low
    low_load = own_rhs[height:] + lax.dynamic_slice_in_dim(rhs_add, low_start, height, 0)
    solved = eliminate(jnp.concatenate([whole_up, load_up[:, None]], 1), width)
    panel = solved[:, :width]
    forward = solved[:, width]
    local_panel = lax.dynamic_slice_in_dim(panel, place * height, height, 1)
    complement = low_rows[:, width:] - update_dot(local_panel.T, panel)
    carried = low_load - dot(local_panel.T, forward)
    own_solved = lax.dynamic_slice_in_dim(forward, place * height, height, 0)
    return own_solved, complement, carried


def ring_gather(piece, axis, count):
    own = lax.axis_index(axis)
    received = [piece]
    for shift in range(1, count):
        received.append(
            lax.ppermute(piece, axis, [(i, (i + shift) % count) for i in range(count)])
        )
    flipped = jnp.stack(received[::-1])
    doubled = jnp.concatenate([flipped, flipped], 0)
    return lax.dynamic_slice_in_dim(doubled, (count - 1 - own) % count, count, 0)


def swap_join(stacked, axis):
    partner = lax.ppermute(stacked, axis, [(0, 1), (1, 0)])
    upper = lax.axis_index(axis) == 1
    first = jnp.where(upper, partner, stacked)
    second = jnp.where(upper, stacked, partner)
    return jnp.stack([first, second])


def gather_front(front, rhs, axes):
    height = front.shape[0] // 2
    size = front.shape[1]
    piece = jnp.concatenate(
        [front[:height].astype(jnp.float32), jnp.pad(rhs[:height], (0, size - height))[None]], 0
    )
    gathered = lax.all_gather(piece, axes, axis=0, tiled=False)
    front_up = gathered[:, :height, :].reshape(-1, size)
    rhs_up = gathered[:, height, :height].reshape(-1)
    return front_up, rhs_up


def per_device(
    latents,
    blocks,
    pattern,
    linear_term,
    leaf_front,
    live_count,
    leaf_map,
    pair_front,
    pair_rhs,
    pair_map,
    quad_front,
    quad_rhs,
    sub_count,
):
    q_id = lax.axis_index("q")
    hi_id = lax.axis_index("hi")
    lo_id = lax.axis_index("lo")
    blk_id = lax.axis_index("blk")
    blk_count = lax.axis_size("blk")
    sub_id = q_id * 4 + hi_id * 2 + lo_id

    pair_up, pair_up_rhs = gather_front(pair_front[0, 0], pair_rhs[0, 0], PAIR)

    interior = latents.shape[2]
    block_width = latents.shape[3]
    live_mask = (jnp.arange(interior) < live_count[0, 0]).astype(jnp.float32)
    masked = latents[0, 0] * live_mask[:, None].astype(jnp.bfloat16)
    block_terms = jnp.einsum(
        "jkab,jb->jka", blocks[0, 0], masked, preferred_element_type=jnp.float32
    )
    onehot = (pattern[0, 0][:, :, None] == jnp.arange(3 * interior)[None, None, :]).astype(
        jnp.float32
    )
    spread = jnp.einsum("jkd,jka->da", onehot, block_terms, precision=exact_setting)
    outward = jnp.stack([spread[interior : 2 * interior], spread[2 * interior :]])
    from_lower, from_upper = halo_exchange(outward, sub_count)
    gradient = (spread[:interior] + from_lower + from_upper - linear_term[0, 0]) * live_mask[
        :, None
    ]
    total_size = interior * block_width
    grad_flat = gradient.reshape(total_size)

    keep_row = jnp.repeat(live_mask, block_width)
    whole_front = leaf_front[0, 0].astype(jnp.float32)
    inner_block = whole_front[:total_size, :total_size] * keep_row[:, None] * keep_row[
        None, :
    ] + jnp.diag(1.0 - keep_row)
    border = whole_front[:total_size, total_size:] * keep_row[:, None]
    corner = whole_front[total_size:, total_size:]
    solved = eliminate(jnp.concatenate([inner_block, border, grad_flat[:, None]], 1), total_size)
    bound_size = corner.shape[0]
    panel = solved[:, :bound_size]
    leaf_solve = solved[:, bound_size]
    leaf_schur = corner - update_dot(panel.T, panel)
    leaf_carry = -dot(panel.T, leaf_solve)

    leaf_packed = jnp.concatenate([leaf_schur, leaf_carry[None, :]], 0)
    leaf_packed, pair_up, pair_up_rhs = lax.optimization_barrier(
        (leaf_packed, pair_up, pair_up_rhs)
    )
    pair_kids = swap_join(ring_gather(leaf_packed, "blk", blk_count), "lo").reshape(
        (-1,) + leaf_packed.shape
    )
    quad_own, pair_kids = lax.optimization_barrier((quad_front[0, 0], pair_kids))
    quad_up, quad_up_rhs = gather_front(quad_own, quad_rhs[0, 0], QUAD)
    pair_maps = lax.dynamic_slice_in_dim(leaf_map, sub_id // 2 * 2, 2, 0).reshape(
        -1, leaf_map.shape[2]
    )
    pair_place = blk_count * lo_id + blk_id
    pair_solve, pair_schur, pair_carry = tree_level(
        pair_up,
        pair_up_rhs,
        pair_front[0, 0].astype(jnp.float32),
        pair_rhs[0, 0],
        pair_kids[:, :bound_size, :],
        pair_kids[:, bound_size, :],
        pair_maps,
        pair_place,
    )

    pair_height = pair_schur.shape[0]
    pass_size = pair_schur.shape[1]
    pair_packed = jnp.concatenate(
        [pair_schur, jnp.pad(pair_carry, (0, pass_size - pair_height))[None]], 0
    )
    pair_packed, quad_up, quad_up_rhs = lax.optimization_barrier(
        (pair_packed, quad_up, quad_up_rhs)
    )
    quad_kids = swap_join(ring_gather(swap_join(pair_packed, "hi"), "blk", blk_count), "lo")
    quad_kids = quad_kids.transpose(2, 0, 1, 3, 4).reshape(2, -1, pair_height + 1, pass_size)
    quad_children = quad_kids[:, :, :pair_height, :].reshape(2, pass_size, pass_size)
    quad_child_rhs = quad_kids[:, :, pair_height, :pair_height].reshape(2, pass_size)
    quad_maps = lax.dynamic_slice_in_dim(pair_map, sub_id // 4 * 2, 2, 0)
    quad_place = blk_count * (hi_id * 2 + lo_id) + blk_id
    quad_solve, upper_schur, upper_rhs = tree_level(
        quad_up,
        quad_up_rhs,
        quad_front[0, 0].astype(jnp.float32),
        quad_rhs[0, 0],
        quad_children,
        quad_child_rhs,
        quad_maps,
        quad_place,
    )
    return (
        grad_flat[None, None],
        leaf_solve[None, None],
        pair_solve[None, None],
        quad_solve[None, None],
        upper_schur[None, None],
        upper_rhs[None, None],
    )


def solution(mesh):
    sub_count = mesh.shape["sub"]
    blk_count = mesh.shape["blk"]
    grid = mesh.devices.reshape(sub_count // 4, 2, 2, blk_count)
    tree_mesh = Mesh(grid, ("q", "hi", "lo", "blk"))
    placed = (
        P(SUB, "blk", None, None),
        P(SUB, "blk", None, None, None, None),
        P(SUB, "blk", None, None),
        P(SUB, "blk", None, None),
        P(SUB, "blk", None, None),
        P(SUB, "blk"),
        P(),
        P(SUB, "blk", None, None),
        P(SUB, "blk", None),
        P(),
        P(SUB, "blk", None, None),
        P(SUB, "blk", None),
    )

    def body(*args):
        return per_device(*args, sub_count=sub_count)

    return jax.shard_map(
        body,
        mesh=tree_mesh,
        in_specs=placed,
        out_specs=(
            P(SUB, "blk", None),
            P(SUB, "blk", None),
            P(SUB, "blk", None),
            P(SUB, "blk", None),
            P(SUB, "blk", None, None),
            P(SUB, "blk", None),
        ),
        check_vma=False,
    )
```

```python
import jax
import jax.numpy as jnp
from jax import lax
from jax.sharding import Mesh
from jax.sharding import PartitionSpec as P

exact_setting = lax.Precision.HIGHEST
SUB = ("q", "hi", "lo")
PAIR = ("lo", "blk")
QUAD = ("hi", "lo", "blk")
STEP = 128


def dot(a, b):
    return jnp.dot(a, b, precision=exact_setting)


def update_dot(a, b):
    return jnp.dot(a, b, precision=lax.Precision.HIGH, preferred_element_type=jnp.float32)


def halo_exchange(outward, count):
    forward = [(i, i + 1) for i in range(count - 1)]
    backward = [(target, source) for source, target in forward]
    from_lower = lax.ppermute(outward[1], SUB, forward)
    from_upper = lax.ppermute(outward[0], SUB, backward)
    return from_lower, from_upper


def eliminate(rows, width):
    tail = rows.shape[1] - width
    solved = []
    rest = rows
    for start in range(0, width, STEP):
        factor = lax.linalg.cholesky(rest[:STEP, :STEP], symmetrize_input=False)
        upper = lax.linalg.triangular_solve(
            factor, rest[:STEP, STEP:], left_side=True, lower=True
        )
        solved.append(upper[:, upper.shape[1] - tail :])
        remaining = rest.shape[0] - STEP
        if remaining:
            rest = rest[STEP:, STEP:] - update_dot(upper[:, :remaining].T, upper)
    return jnp.concatenate(solved, 0)


def assemble_add(children, child_rhs, maps, total_blocks, low_start, height):
    count, size = children.shape[0], children.shape[1]
    blocks = maps.shape[1]
    width = size // blocks
    onehot = (maps[:, :, None] == jnp.arange(total_blocks)[None, None, :]).astype(jnp.float32)
    pair_weights = (onehot[:, :, None, :, None] * onehot[:, None, :, None, :]).reshape(
        count * blocks * blocks, total_blocks * total_blocks
    )
    tiles = (
        children.reshape(count, blocks, width, blocks, width)
        .transpose(0, 1, 3, 2, 4)
        .reshape(count * blocks * blocks, width * width)
    )
    weights = pair_weights.T
    half = total_blocks // 2

    def place_rows(chosen):
        rows = dot(chosen, tiles).reshape(-1, total_blocks, width, width)
        return rows.transpose(0, 2, 1, 3).reshape(-1, total_blocks * width)

    placed_up = place_rows(weights[: half * total_blocks])
    low_block = lax.dynamic_slice_in_dim(
        weights, (low_start // width) * total_blocks, total_blocks, 0
    )
    placed_low = lax.dynamic_slice_in_dim(
        place_rows(low_block), low_start % width, height, 0
    )
    rhs_add = jnp.einsum(
        "cjm,cja->ma", onehot, child_rhs.reshape(count, blocks, width), precision=exact_setting
    ).reshape(total_blocks * width)
    return placed_up, placed_low, rhs_add


def tree_level(front_up, rhs_up, own_front, own_rhs, children, child_rhs, maps, place):
    height = own_front.shape[0] // 2
    size = own_front.shape[1]
    width = size // 2
    total_blocks = size // (children.shape[1] // maps.shape[1])
    low_start = width + place * height
    placed_up, placed_low, rhs_add = assemble_add(
        children, child_rhs, maps, total_blocks, low_start, height
    )
    whole_up = front_up + placed_up
    load_up = rhs_up + rhs_add[:width]
    low_rows = own_front[height:] + placed_low
    low_load = own_rhs[height:] + lax.dynamic_slice_in_dim(rhs_add, low_start, height, 0)
    solved = eliminate(jnp.concatenate([whole_up, load_up[:, None]], 1), width)
    panel = solved[:, :width]
    forward = solved[:, width]
    local_panel = lax.dynamic_slice_in_dim(panel, place * height, height, 1)
    complement = low_rows[:, width:] - update_dot(local_panel.T, panel)
    carried = low_load - dot(local_panel.T, forward)
    own_solved = lax.dynamic_slice_in_dim(forward, place * height, height, 0)
    return own_solved, complement, carried


def ring_gather(piece, axis, count):
    own = lax.axis_index(axis)
    received = [piece]
    for shift in range(1, count):
        received.append(
            lax.ppermute(piece, axis, [(i, (i + shift) % count) for i in range(count)])
        )
    flipped = jnp.stack(received[::-1])
    doubled = jnp.concatenate([flipped, flipped], 0)
    return lax.dynamic_slice_in_dim(doubled, (count - 1 - own) % count, count, 0)


def swap_join(stacked, axis):
    partner = lax.ppermute(stacked, axis, [(0, 1), (1, 0)])
    upper = lax.axis_index(axis) == 1
    first = jnp.where(upper, partner, stacked)
    second = jnp.where(upper, stacked, partner)
    return jnp.stack([first, second])


def gather_front(front, rhs, axes):
    height = front.shape[0] // 2
    size = front.shape[1]
    piece = jnp.concatenate(
        [front[:height].astype(jnp.float32), jnp.pad(rhs[:height], (0, size - height))[None]], 0
    )
    gathered = lax.all_gather(piece, axes, axis=0, tiled=False)
    front_up = gathered[:, :height, :].reshape(-1, size)
    rhs_up = gathered[:, height, :height].reshape(-1)
    return front_up, rhs_up


def per_device(
    latents,
    blocks,
    pattern,
    linear_term,
    leaf_front,
    live_count,
    leaf_map,
    pair_front,
    pair_rhs,
    pair_map,
    quad_front,
    quad_rhs,
    sub_count,
):
    q_id = lax.axis_index("q")
    hi_id = lax.axis_index("hi")
    lo_id = lax.axis_index("lo")
    blk_id = lax.axis_index("blk")
    blk_count = lax.axis_size("blk")
    sub_id = q_id * 4 + hi_id * 2 + lo_id

    pair_up, pair_up_rhs = gather_front(pair_front[0, 0], pair_rhs[0, 0], PAIR)

    interior = latents.shape[2]
    block_width = latents.shape[3]
    live_mask = (jnp.arange(interior) < live_count[0, 0]).astype(jnp.float32)
    masked = latents[0, 0] * live_mask[:, None].astype(jnp.bfloat16)
    block_terms = jnp.einsum(
        "jkab,jb->jka", blocks[0, 0], masked, preferred_element_type=jnp.float32
    )
    onehot = (pattern[0, 0][:, :, None] == jnp.arange(3 * interior)[None, None, :]).astype(
        jnp.float32
    )
    spread = jnp.einsum("jkd,jka->da", onehot, block_terms, precision=exact_setting)
    outward = jnp.stack([spread[interior : 2 * interior], spread[2 * interior :]])
    from_lower, from_upper = halo_exchange(outward, sub_count)
    gradient = (spread[:interior] + from_lower + from_upper - linear_term[0, 0]) * live_mask[
        :, None
    ]
    total_size = interior * block_width
    grad_flat = gradient.reshape(total_size)

    keep_row = jnp.repeat(live_mask, block_width)
    whole_front = leaf_front[0, 0].astype(jnp.float32)
    inner_block = whole_front[:total_size, :total_size] * keep_row[:, None] * keep_row[
        None, :
    ] + jnp.diag(1.0 - keep_row)
    border = whole_front[:total_size, total_size:] * keep_row[:, None]
    corner = whole_front[total_size:, total_size:]
    solved = eliminate(jnp.concatenate([inner_block, border, grad_flat[:, None]], 1), total_size)
    bound_size = corner.shape[0]
    panel = solved[:, :bound_size]
    leaf_solve = solved[:, bound_size]
    leaf_schur = corner - update_dot(panel.T, panel)
    leaf_carry = -dot(panel.T, leaf_solve)

    leaf_packed = jnp.concatenate([leaf_schur, leaf_carry[None, :]], 0)
    leaf_packed, pair_up, pair_up_rhs = lax.optimization_barrier(
        (leaf_packed, pair_up, pair_up_rhs)
    )
    own_group = ring_gather(leaf_packed, "blk", blk_count)
    partner_group = lax.ppermute(own_group, "lo", [(0, 1), (1, 0)])
    pair_kids = jnp.concatenate([own_group, partner_group], 0)
    quad_own, pair_kids = lax.optimization_barrier((quad_front[0, 0], pair_kids))
    quad_up, quad_up_rhs = gather_front(quad_own, quad_rhs[0, 0], QUAD)
    pair_maps = lax.dynamic_slice_in_dim(leaf_map, sub_id // 2 * 2, 2, 0)
    pair_maps = jnp.where(lo_id == 1, pair_maps[::-1], pair_maps).reshape(-1, leaf_map.shape[2])
    pair_place = blk_count * lo_id + blk_id
    pair_solve, pair_schur, pair_carry = tree_level(
        pair_up,
        pair_up_rhs,
        pair_front[0, 0].astype(jnp.float32),
        pair_rhs[0, 0],
        pair_kids[:, :bound_size, :],
        pair_kids[:, bound_size, :],
        pair_maps,
        pair_place,
    )

    pair_height = pair_schur.shape[0]
    pass_size = pair_schur.shape[1]
    pair_packed = jnp.concatenate(
        [pair_schur, jnp.pad(pair_carry, (0, pass_size - pair_height))[None]], 0
    )
    pair_packed, quad_up, quad_up_rhs = lax.optimization_barrier(
        (pair_packed, quad_up, quad_up_rhs)
    )
    quad_kids = swap_join(ring_gather(swap_join(pair_packed, "hi"), "blk", blk_count), "lo")
    quad_kids = quad_kids.transpose(2, 0, 1, 3, 4).reshape(2, -1, pair_height + 1, pass_size)
    quad_children = quad_kids[:, :, :pair_height, :].reshape(2, pass_size, pass_size)
    quad_child_rhs = quad_kids[:, :, pair_height, :pair_height].reshape(2, pass_size)
    quad_maps = lax.dynamic_slice_in_dim(pair_map, sub_id // 4 * 2, 2, 0)
    quad_place = blk_count * (hi_id * 2 + lo_id) + blk_id
    quad_solve, upper_schur, upper_rhs = tree_level(
        quad_up,
        quad_up_rhs,
        quad_front[0, 0].astype(jnp.float32),
        quad_rhs[0, 0],
        quad_children,
        quad_child_rhs,
        quad_maps,
        quad_place,
    )
    return (
        grad_flat[None, None],
        leaf_solve[None, None],
        pair_solve[None, None],
        quad_solve[None, None],
        upper_schur[None, None],
        upper_rhs[None, None],
    )


def solution(mesh):
    sub_count = mesh.shape["sub"]
    blk_count = mesh.shape["blk"]
    grid = mesh.devices.reshape(sub_count // 4, 2, 2, blk_count)
    tree_mesh = Mesh(grid, ("q", "hi", "lo", "blk"))
    placed = (
        P(SUB, "blk", None, None),
        P(SUB, "blk", None, None, None, None),
        P(SUB, "blk", None, None),
        P(SUB, "blk", None, None),
        P(SUB, "blk", None, None),
        P(SUB, "blk"),
        P(),
        P(SUB, "blk", None, None),
        P(SUB, "blk", None),
        P(),
        P(SUB, "blk", None, None),
        P(SUB, "blk", None),
    )

    def body(*args):
        return per_device(*args, sub_count=sub_count)

    return jax.shard_map(
        body,
        mesh=tree_mesh,
        in_specs=placed,
        out_specs=(
            P(SUB, "blk", None),
            P(SUB, "blk", None),
            P(SUB, "blk", None),
            P(SUB, "blk", None),
            P(SUB, "blk", None, None),
            P(SUB, "blk", None),
        ),
        check_vma=False,
    )
```

```python
import jax
import jax.numpy as jnp
from jax import lax
from jax.sharding import Mesh
from jax.sharding import PartitionSpec as P

exact_setting = lax.Precision.HIGHEST
SUB = ("q", "hi", "lo")
PAIR = ("lo", "blk")
QUAD = ("hi", "lo", "blk")
STEP = 128


def dot(a, b):
    return jnp.dot(a, b, precision=exact_setting)


def update_dot(a, b):
    return jnp.dot(a, b, precision=lax.Precision.HIGH, preferred_element_type=jnp.float32)


def halo_exchange(outward, count):
    forward = [(i, i + 1) for i in range(count - 1)]
    backward = [(target, source) for source, target in forward]
    from_lower = lax.ppermute(outward[1], SUB, forward)
    from_upper = lax.ppermute(outward[0], SUB, backward)
    return from_lower, from_upper


def eliminate(rows, width):
    tail = rows.shape[1] - width
    solved = []
    rest = rows
    for start in range(0, width, STEP):
        factor = lax.linalg.cholesky(rest[:STEP, :STEP], symmetrize_input=False)
        upper = lax.linalg.triangular_solve(
            factor, rest[:STEP, STEP:], left_side=True, lower=True
        )
        solved.append(upper[:, upper.shape[1] - tail :])
        remaining = rest.shape[0] - STEP
        if remaining:
            rest = rest[STEP:, STEP:] - update_dot(upper[:, :remaining].T, upper)
    return jnp.concatenate(solved, 0)


def assemble_add(children, child_rhs, maps, row_maps, total_blocks, low_start, height):
    count, size = children.shape[0], children.shape[1]
    blocks = maps.shape[1]
    width = size // blocks
    onehot = (maps[:, :, None] == jnp.arange(total_blocks)[None, None, :]).astype(jnp.float32)
    row_onehot = (row_maps[:, :, None] == jnp.arange(total_blocks)[None, None, :]).astype(
        jnp.float32
    )
    pair_weights = (row_onehot[:, :, None, :, None] * onehot[:, None, :, None, :]).reshape(
        count * blocks * blocks, total_blocks * total_blocks
    )
    tiles = (
        children.reshape(count, blocks, width, blocks, width)
        .transpose(0, 1, 3, 2, 4)
        .reshape(count * blocks * blocks, width * width)
    )
    weights = pair_weights.T
    half = total_blocks // 2

    def place_rows(chosen):
        rows = dot(chosen, tiles).reshape(-1, total_blocks, width, width)
        return rows.transpose(0, 2, 1, 3).reshape(-1, total_blocks * width)

    placed_up = place_rows(weights[: half * total_blocks])
    low_block = lax.dynamic_slice_in_dim(
        weights, (low_start // width) * total_blocks, total_blocks, 0
    )
    placed_low = lax.dynamic_slice_in_dim(
        place_rows(low_block), low_start % width, height, 0
    )
    rhs_add = jnp.einsum(
        "cjm,cja->ma", row_onehot, child_rhs.reshape(count, blocks, width), precision=exact_setting
    ).reshape(total_blocks * width)
    return placed_up, placed_low, rhs_add


def tree_level(front_up, rhs_up, own_front, own_rhs, children, child_rhs, maps, row_maps, place):
    height = own_front.shape[0] // 2
    size = own_front.shape[1]
    width = size // 2
    total_blocks = size // (children.shape[1] // maps.shape[1])
    low_start = width + place * height
    placed_up, placed_low, rhs_add = assemble_add(
        children, child_rhs, maps, row_maps, total_blocks, low_start, height
    )
    whole_up = front_up + placed_up
    load_up = rhs_up + rhs_add[:width]
    low_rows = own_front[height:] + placed_low
    low_load = own_rhs[height:] + lax.dynamic_slice_in_dim(rhs_add, low_start, height, 0)
    solved = eliminate(jnp.concatenate([whole_up, load_up[:, None]], 1), width)
    panel = solved[:, :width]
    forward = solved[:, width]
    local_panel = lax.dynamic_slice_in_dim(panel, place * height, height, 1)
    complement = low_rows[:, width:] - update_dot(local_panel.T, panel)
    carried = low_load - dot(local_panel.T, forward)
    own_solved = lax.dynamic_slice_in_dim(forward, place * height, height, 0)
    return own_solved, complement, carried


def ring_gather(piece, axis, count):
    own = lax.axis_index(axis)
    received = [piece]
    for shift in range(1, count):
        received.append(
            lax.ppermute(piece, axis, [(i, (i + shift) % count) for i in range(count)])
        )
    flipped = jnp.stack(received[::-1])
    doubled = jnp.concatenate([flipped, flipped], 0)
    return lax.dynamic_slice_in_dim(doubled, (count - 1 - own) % count, count, 0)


def swap_join(stacked, axis):
    partner = lax.ppermute(stacked, axis, [(0, 1), (1, 0)])
    upper = lax.axis_index(axis) == 1
    first = jnp.where(upper, partner, stacked)
    second = jnp.where(upper, stacked, partner)
    return jnp.stack([first, second])


def gather_front(front, rhs, axes):
    height = front.shape[0] // 2
    size = front.shape[1]
    piece = jnp.concatenate(
        [front[:height].astype(jnp.float32), jnp.pad(rhs[:height], (0, size - height))[None]], 0
    )
    gathered = lax.all_gather(piece, axes, axis=0, tiled=False)
    front_up = gathered[:, :height, :].reshape(-1, size)
    rhs_up = gathered[:, height, :height].reshape(-1)
    return front_up, rhs_up


def per_device(
    latents,
    blocks,
    pattern,
    linear_term,
    leaf_front,
    live_count,
    leaf_map,
    pair_front,
    pair_rhs,
    pair_map,
    quad_front,
    quad_rhs,
    sub_count,
):
    q_id = lax.axis_index("q")
    hi_id = lax.axis_index("hi")
    lo_id = lax.axis_index("lo")
    blk_id = lax.axis_index("blk")
    blk_count = lax.axis_size("blk")
    sub_id = q_id * 4 + hi_id * 2 + lo_id

    pair_up, pair_up_rhs = gather_front(pair_front[0, 0], pair_rhs[0, 0], PAIR)

    interior = latents.shape[2]
    block_width = latents.shape[3]
    live_mask = (jnp.arange(interior) < live_count[0, 0]).astype(jnp.float32)
    masked = latents[0, 0] * live_mask[:, None].astype(jnp.bfloat16)
    block_terms = jnp.einsum(
        "jkab,jb->jka", blocks[0, 0], masked, preferred_element_type=jnp.float32
    )
    onehot = (pattern[0, 0][:, :, None] == jnp.arange(3 * interior)[None, None, :]).astype(
        jnp.float32
    )
    spread = jnp.einsum("jkd,jka->da", onehot, block_terms, precision=exact_setting)
    outward = jnp.stack([spread[interior : 2 * interior], spread[2 * interior :]])
    from_lower, from_upper = halo_exchange(outward, sub_count)
    gradient = (spread[:interior] + from_lower + from_upper - linear_term[0, 0]) * live_mask[
        :, None
    ]
    total_size = interior * block_width
    grad_flat = gradient.reshape(total_size)

    keep_row = jnp.repeat(live_mask, block_width)
    whole_front = leaf_front[0, 0].astype(jnp.float32)
    inner_block = whole_front[:total_size, :total_size] * keep_row[:, None] * keep_row[
        None, :
    ] + jnp.diag(1.0 - keep_row)
    border = whole_front[:total_size, total_size:] * keep_row[:, None]
    corner = whole_front[total_size:, total_size:]
    solved = eliminate(jnp.concatenate([inner_block, border, grad_flat[:, None]], 1), total_size)
    bound_size = corner.shape[0]
    panel = solved[:, :bound_size]
    leaf_solve = solved[:, bound_size]
    leaf_schur = corner - update_dot(panel.T, panel)
    leaf_carry = -dot(panel.T, leaf_solve)

    leaf_packed = jnp.concatenate([leaf_schur, leaf_carry[None, :]], 0)
    leaf_packed, pair_up, pair_up_rhs = lax.optimization_barrier(
        (leaf_packed, pair_up, pair_up_rhs)
    )
    own_group = ring_gather(leaf_packed, "blk", blk_count)
    partner_group = lax.ppermute(own_group, "lo", [(0, 1), (1, 0)])
    pair_kids = jnp.concatenate([own_group, partner_group], 0)
    quad_own, pair_kids = lax.optimization_barrier((quad_front[0, 0], pair_kids))
    quad_up, quad_up_rhs = gather_front(quad_own, quad_rhs[0, 0], QUAD)
    pair_maps = lax.dynamic_slice_in_dim(leaf_map, sub_id // 2 * 2, 2, 0)
    pair_maps = jnp.where(lo_id == 1, pair_maps[::-1], pair_maps).reshape(-1, leaf_map.shape[2])
    pair_place = blk_count * lo_id + blk_id
    pair_solve, pair_schur, pair_carry = tree_level(
        pair_up,
        pair_up_rhs,
        pair_front[0, 0].astype(jnp.float32),
        pair_rhs[0, 0],
        pair_kids[:, :bound_size, :],
        pair_kids[:, bound_size, :],
        pair_maps,
        pair_maps,
        pair_place,
    )

    pair_height = pair_schur.shape[0]
    pass_size = pair_schur.shape[1]
    pair_packed = jnp.concatenate(
        [pair_schur, jnp.pad(pair_carry, (0, pass_size - pair_height))[None]], 0
    )
    pair_packed, quad_up, quad_up_rhs = lax.optimization_barrier(
        (pair_packed, quad_up, quad_up_rhs)
    )
    quad_inner = ring_gather(swap_join(pair_packed, "hi"), "blk", blk_count)
    quad_kids = jnp.stack([quad_inner, lax.ppermute(quad_inner, "lo", [(0, 1), (1, 0)])])
    quad_kids = quad_kids.transpose(2, 0, 1, 3, 4).reshape(2, -1, pair_height + 1, pass_size)
    quad_children = quad_kids[:, :, :pair_height, :].reshape(2, pass_size, pass_size)
    quad_child_rhs = quad_kids[:, :, pair_height, :pair_height].reshape(2, pass_size)
    quad_maps = lax.dynamic_slice_in_dim(pair_map, sub_id // 4 * 2, 2, 0)
    quad_place = blk_count * (hi_id * 2 + lo_id) + blk_id
    quad_solve, upper_schur, upper_rhs = tree_level(
        quad_up,
        quad_up_rhs,
        quad_front[0, 0].astype(jnp.float32),
        quad_rhs[0, 0],
        quad_children,
        quad_child_rhs,
        quad_maps,
        jnp.where(lo_id == 1, jnp.roll(quad_maps, 2, axis=1), quad_maps),
        quad_place,
    )
    return (
        grad_flat[None, None],
        leaf_solve[None, None],
        pair_solve[None, None],
        quad_solve[None, None],
        upper_schur[None, None],
        upper_rhs[None, None],
    )


def solution(mesh):
    sub_count = mesh.shape["sub"]
    blk_count = mesh.shape["blk"]
    grid = mesh.devices.reshape(sub_count // 4, 2, 2, blk_count)
    tree_mesh = Mesh(grid, ("q", "hi", "lo", "blk"))
    placed = (
        P(SUB, "blk", None, None),
        P(SUB, "blk", None, None, None, None),
        P(SUB, "blk", None, None),
        P(SUB, "blk", None, None),
        P(SUB, "blk", None, None),
        P(SUB, "blk"),
        P(),
        P(SUB, "blk", None, None),
        P(SUB, "blk", None),
        P(),
        P(SUB, "blk", None, None),
        P(SUB, "blk", None),
    )

    def body(*args):
        return per_device(*args, sub_count=sub_count)

    return jax.shard_map(
        body,
        mesh=tree_mesh,
        in_specs=placed,
        out_specs=(
            P(SUB, "blk", None),
            P(SUB, "blk", None),
            P(SUB, "blk", None),
            P(SUB, "blk", None),
            P(SUB, "blk", None, None),
            P(SUB, "blk", None),
        ),
        check_vma=False,
    )
```
